256 devices in a mesh: section: 8 (over x, core), dp: 32 (over y, z).
Axes of the slice: x: 4, y: 4, z: 8, core: 2. Of those that a mesh axis runs over, the one named last changes fastest.
Arguments:
- resid_in: bfloat16 [4, 1024, 2048], P(None, 'dp'), may hold values from -10 to 10
- dest_row: int32 [4, 1024], replicated, may hold values from 0 to 1023, as said below
- doc_ids: int32 [4, 1024], P(None, 'dp'), may hold values from 0 to 1023, as said below
- cotangent: bfloat16 [4, 1024, 2048], P(None, 'dp'), may hold values from -0.119628906 to 0.119628906
- gain: float32 [8, 2048], P('section'), may hold values from 0.5 to 1.5
- steer: float32 [8, 2048], P('section'), may hold values from -3 to 3
- w_query: bfloat16 [8, 2048, 1024], P('section', 'dp'), may hold values from -1 to 1
- w_keyval: bfloat16 [8, 2048, 512], P('section', 'dp'), may hold values from -1 to 1
- w_out: bfloat16 [8, 1024, 2048], P('section', None, 'dp'), may hold values from -0.1875 to 0.1875
Outputs:
- hidden_out: bfloat16 [8, 4, 1024, 2048], P('section', None, 'dp')
- grad_steer: float32 [8, 2048], P('section')
The draws below stay inside these ranges and needn't reach their ends.
Inputs may be any that keep to these rules, and one draw needn't show every extreme that they name: Each row of dest_row is a permutation of 0 to 1023. Counting the tokens of one aligned block of 32 input tokens that go to one aligned block of 32 packed rows, no count exceeds 2, and some reach it in every micro-batch. doc_ids never falls along a row; every value is a row index r at which doc_ids equals r; each aligned block of 32 rows begins a document, so no document crosses such a block.
All inputs are finite; a program needn't handle non-finite values.
Results may differ from the reference program's by a relative error of at most 0.02.
Values may be sent and summed in bfloat16 or wider, within the bound.
No kernel may reach another device: no remote copies, remote signals or barrier semaphores. Data moves between devices by JAX's collectives and lax.ppermute only.
A program may use at most 64 MiB of HBM per device.

```python
import jax
import jax.numpy as jnp
from jax import lax

D = 2048
HD = 64
QH = 16
KVH = 4
MICRO = 4
TOK_MB = 32
SECTIONS = 8
TOKENS = 1024
N_SECTION = 8


def plan_micro(key):
    group_count = TOKENS // TOK_MB
    base_count = TOK_MB // group_count
    key_sign, key_cols, key_rows, key_dest = jax.random.split(key, 4)
    signs = jnp.where(jax.random.permutation(key_sign, group_count) < group_count // 2, 1, -1).astype(jnp.int32)
    profile = base_count + signs
    columns = jax.random.permutation(key_cols, group_count).astype(jnp.int32)
    source_ids = jnp.arange(group_count, dtype=jnp.int32)[:, None]
    counts = profile[(columns[None, :] - source_ids) % group_count]
    ends = jnp.cumsum(counts, axis=1)
    starts = ends - counts
    slot_ids = jnp.arange(TOK_MB, dtype=jnp.int32)
    target_sorted = jnp.sum((ends[:, None, :] <= slot_ids[None, :, None]).astype(jnp.int32), axis=2)
    rank_sorted = slot_ids[None, :] - jnp.take_along_axis(starts, target_sorted, axis=1)
    offsets = jnp.cumsum(counts, axis=0) - counts
    offset_sorted = jnp.take_along_axis(offsets, target_sorted, axis=1) + rank_sorted
    row_keys = jax.random.split(key_rows, group_count)
    shuffles = jax.vmap(lambda sub_key: jax.random.permutation(sub_key, TOK_MB))(row_keys).astype(jnp.int32)
    dest_keys = jax.random.split(key_dest, group_count)
    dest_shuffles = jax.vmap(lambda sub_key: jax.random.permutation(sub_key, TOK_MB))(dest_keys).astype(jnp.int32)
    final_offset = dest_shuffles[target_sorted, offset_sorted]
    dest_sorted = target_sorted * TOK_MB + final_offset
    result = jnp.zeros((group_count, TOK_MB), jnp.int32)
    result = result.at[source_ids, shuffles].set(dest_sorted)
    return result.reshape(TOKENS).astype(jnp.int32)


def draw_dest_row(key, part):
    micro_keys = jax.random.split(jax.random.fold_in(key, 11), MICRO)
    return jax.vmap(plan_micro)(micro_keys).astype(jnp.int32)


def draw_doc_ids(key, part):
    flags = jax.random.randint(jax.random.fold_in(key, 23), (MICRO, TOKENS), 0, 16) == 0
    global_rows = jnp.arange(TOKENS, dtype=jnp.int32)
    flags = flags | (global_rows % TOK_MB == 0)[None, :]
    marks = jnp.where(flags, global_rows[None, :], -1)
    return lax.cummax(marks, axis=1).astype(jnp.int32)


def drawn_weights(key, salt, column_count):
    shape = (SECTIONS, D, column_count)
    result = jnp.clip(jax.random.normal(jax.random.fold_in(key, salt), shape, jnp.float32), -6.0, 6.0) * D ** (-0.5)
    return result.astype(jnp.bfloat16)


def draw_w_query(key, part):
    return drawn_weights(key, 41, QH * HD)


def draw_w_keyval(key, part):
    return drawn_weights(key, 43, 2 * KVH * HD)


def draw_resid_in(key, part):
    shape = (MICRO, TOKENS, D)
    result = jnp.clip(jax.random.normal(jax.random.fold_in(key, 31), shape, jnp.float32), -6.0, 6.0)
    return result.astype(jnp.bfloat16)


def block_scale(stream_key, dims, pieces, smallest, largest):
    level = 1.0
    for axis_at, shards_of in pieces:
        steps = jax.random.uniform(jax.random.fold_in(jax.random.fold_in(stream_key, 6), axis_at), (shards_of,), jnp.float32, smallest / len(pieces), largest / len(pieces))
        level = level * jnp.repeat(jnp.exp(steps), dims[axis_at] // shards_of).reshape((-1,) + (1,) * (len(dims) - 1 - axis_at))
    return level


def gaussian(stream_key, extent, width, limit, shards=(), held_as=jnp.bfloat16):
    values = jax.random.normal(stream_key, extent, jnp.float32) * width
    if len(shards) > 0:
        values = block_scale(stream_key, extent, shards, -0.22, 0.18) * values
    return jnp.clip(values, min=-limit, max=limit).astype(held_as)


def setup_inputs(seed: int = 0) -> dict:
    key_of = jax.random.split(jax.random.key(seed), 10)
    resid_in = draw_resid_in(jax.random.fold_in(key_of[9], 71), 0)
    dest_row = draw_dest_row(jax.random.fold_in(key_of[9], 71), 0)
    doc_ids = draw_doc_ids(jax.random.fold_in(key_of[9], 71), 0)
    cotangent = gaussian(key_of[3], (MICRO, TOKENS, D), 0.02, 0.119628906, ((1, 32),))
    gain = jnp.clip(1.0 + 0.1 * jax.random.normal(key_of[4], (SECTIONS, D), jnp.float32), 0.5, 1.5)
    steer = gaussian(key_of[5], (SECTIONS, D), 0.5, 3.0, ((0, 8),), jnp.float32)
    w_query = draw_w_query(jax.random.fold_in(key_of[9], 71), 0)
    w_keyval = draw_w_keyval(jax.random.fold_in(key_of[9], 71), 0)
    w_out = gaussian(key_of[8], (SECTIONS, QH * HD, D), (QH * HD) ** -0.5, 0.1875, ((0, 8), (2, 32)))
    return dict(resid_in=resid_in, dest_row=dest_row, doc_ids=doc_ids, cotangent=cotangent, gain=gain, steer=steer, w_query=w_query, w_keyval=w_keyval, w_out=w_out)


ROPE_BASE = 500000.0
EPSILON = 1e-05
MASKED = -1e+30

def rotate(values, positions):
    half_size = values.shape[-1] // 2
    freq_index = jnp.arange(half_size, dtype=jnp.float32)
    inverse = ROPE_BASE ** (-2.0 * freq_index / values.shape[-1])
    angles = positions.astype(jnp.float32)[:, None] * inverse[None, :]
    cosine = jnp.cos(angles)[:, None, :]
    sine_part = jnp.sin(angles)[:, None, :]
    first_half = values[..., :half_size]
    second = values[..., half_size:]
    return jnp.concatenate([first_half * cosine - second * sine_part, second * cosine + first_half * sine_part], axis=-1)

def layer(hidden_in, steering, gain_row, w_query, w_keyval, w_out, positions, documents):
    row_count = hidden_in.shape[0]
    head_size = HD
    kv_heads = w_keyval.shape[1] // (2 * head_size)
    query_heads = w_query.shape[1] // head_size
    group_size = query_heads // kv_heads
    residual = hidden_in.astype(jnp.float32) + steering
    normed = (residual * lax.rsqrt(lax.optimization_barrier(jnp.mean(residual * residual, axis=-1, keepdims=True)) + EPSILON) * gain_row).astype(jnp.bfloat16)
    queries = jnp.dot(normed, w_query, preferred_element_type=jnp.float32).reshape(row_count, query_heads, head_size)
    keyval = jnp.dot(normed, w_keyval, preferred_element_type=jnp.float32)
    key_rows = rotate(keyval[:, :kv_heads * head_size].reshape(row_count, kv_heads, head_size), positions).astype(jnp.bfloat16)
    values = keyval[:, kv_heads * head_size:].reshape(row_count, kv_heads, head_size).astype(jnp.bfloat16)
    queries = rotate(queries, positions).astype(jnp.bfloat16).reshape(row_count, kv_heads, group_size, head_size)
    scores = jnp.einsum('rkgd,skd->kgrs', queries.astype(jnp.float32), key_rows.astype(jnp.float32)) * head_size ** (-0.5)
    row_index = jnp.arange(row_count)
    allowed = (documents[:, None] == documents[None, :]) & (row_index[:, None] >= row_index[None, :])
    scores = jnp.where(allowed[None, None], scores, MASKED)
    peak = lax.optimization_barrier(jnp.max(scores, axis=-1, keepdims=True))
    weights = jnp.exp(scores - peak)
    weights = (weights / lax.optimization_barrier(jnp.sum(weights, axis=-1, keepdims=True))).astype(jnp.bfloat16)
    mixed_heads = jnp.einsum('kgrs,skd->rkgd', weights.astype(jnp.float32), values.astype(jnp.float32)).astype(jnp.bfloat16)
    mixed_heads = mixed_heads.reshape(row_count, query_heads * head_size)
    return (residual + jnp.dot(mixed_heads, w_out, preferred_element_type=jnp.float32)).astype(jnp.bfloat16)

def partial_layer(gain_row, w_query, w_keyval, w_out, positions, documents):

    def local(hidden_in, steering):
        return layer(hidden_in, steering, gain_row, w_query, w_keyval, w_out, positions, documents)
    return local

def reference(resid_in, dest_row, doc_ids, cotangent, gain, steer, w_query, w_keyval, w_out):
    token_count = resid_in.shape[1]
    grads = jnp.zeros(steer.shape, jnp.float32)
    section_outputs = []
    for micro_idx in range(MICRO):
        grouped = jnp.zeros_like(resid_in[micro_idx]).at[dest_row[micro_idx]].set(resid_in[micro_idx])
        documents = doc_ids[micro_idx]
        positions = jnp.arange(token_count, dtype=jnp.int32) - documents
        hidden = grouped
        inputs_kept = []
        per_micro = []
        for section_idx in range(N_SECTION):
            inputs_kept.append(hidden)
            hidden = layer(hidden, steer[section_idx], gain[section_idx], w_query[section_idx], w_keyval[section_idx], w_out[section_idx], positions, documents)
            per_micro.append(hidden)
        section_outputs.append(jnp.stack(per_micro))
        upstream = cotangent[micro_idx]
        for section_idx in reversed(range(N_SECTION)):
            local = partial_layer(gain[section_idx], w_query[section_idx], w_keyval[section_idx], w_out[section_idx], positions, documents)
            unused, pullback = jax.vjp(local, inputs_kept[section_idx], steer[section_idx])
            upstream, steer_part = pullback(upstream)
            grads = grads.at[section_idx].add(steer_part)
    hidden_out = jnp.stack(section_outputs, axis=1)
    return (hidden_out, grads)
```

```python
import jax
import jax.numpy as jnp
from jax import lax
from jax.sharding import PartitionSpec as P

HD = 64


ROPE_BASE = 500000.0
EPSILON = 1e-05
MASKED = -1e30


def rotate(values, positions):
    half_size = values.shape[-1] // 2
    freq_index = jnp.arange(half_size, dtype=jnp.float32)
    inverse = ROPE_BASE ** (-2.0 * freq_index / values.shape[-1])
    angles = positions.astype(jnp.float32)[..., None] * inverse
    cosine = jnp.cos(angles)[..., None, :]
    sine_part = jnp.sin(angles)[..., None, :]
    first_half = values[..., :half_size]
    second = values[..., half_size:]
    return jnp.concatenate(
        [first_half * cosine - second * sine_part, second * cosine + first_half * sine_part],
        axis=-1,
    )


def layer(hidden_in, steering, gain_row, w_query, w_keyval, w_out, positions, documents):
    micro_count, row_count, width = hidden_in.shape
    head_size = HD
    kv_heads = w_keyval.shape[1] // (2 * head_size)
    query_heads = w_query.shape[1] // head_size
    group_size = query_heads // kv_heads
    residual = hidden_in.astype(jnp.float32) + steering
    normed = (
        residual
        * lax.rsqrt(jnp.mean(residual * residual, axis=-1, keepdims=True) + EPSILON)
        * gain_row
    ).astype(jnp.bfloat16)
    flat = normed.reshape(micro_count * row_count, width)
    queries = jnp.dot(flat, w_query, preferred_element_type=jnp.float32).reshape(
        micro_count, row_count, query_heads, head_size
    )
    keyval = jnp.dot(flat, w_keyval, preferred_element_type=jnp.float32).reshape(
        micro_count, row_count, 2 * kv_heads * head_size
    )
    key_rows = rotate(
        keyval[..., : kv_heads * head_size].reshape(micro_count, row_count, kv_heads, head_size),
        positions,
    ).astype(jnp.bfloat16)
    values = (
        keyval[..., kv_heads * head_size :]
        .reshape(micro_count, row_count, kv_heads, head_size)
        .astype(jnp.bfloat16)
    )
    queries = (
        rotate(queries, positions)
        .astype(jnp.bfloat16)
        .reshape(micro_count, row_count, kv_heads, group_size, head_size)
    )
    scores = jnp.einsum(
        "mrkgd,mskd->mkgrs", queries, key_rows, preferred_element_type=jnp.float32
    ) * head_size ** (-0.5)
    row_index = jnp.arange(row_count)
    allowed = (documents[:, :, None] == documents[:, None, :]) & (
        row_index[:, None] >= row_index[None, :]
    )
    scores = jnp.where(allowed[:, None, None], scores, MASKED)
    peak = jnp.max(scores, axis=-1, keepdims=True)
    weights = jnp.exp(scores - peak)
    weights = (weights / jnp.sum(weights, axis=-1, keepdims=True)).astype(jnp.bfloat16)
    mixed_heads = jnp.einsum(
        "mkgrs,mskd->mrkgd", weights, values, preferred_element_type=jnp.float32
    ).astype(jnp.bfloat16)
    mixed_heads = mixed_heads.reshape(micro_count * row_count, query_heads * head_size)
    projected = jnp.dot(mixed_heads, w_out, preferred_element_type=jnp.float32).reshape(
        micro_count, row_count, width
    )
    return (residual + projected).astype(jnp.bfloat16)


def plan_slots(target, device, row_count, capacity, dp_count):
    target_grid = target.reshape(dp_count, row_count)
    target_dev = target_grid // row_count
    target_off = target_grid % row_count
    row_order = jnp.arange(row_count, dtype=jnp.int32)
    matching = target_dev[:, :, None] == target_dev[:, None, :]
    earlier = row_order[None, :] < row_order[:, None]
    rank_ids = jnp.sum((matching & earlier[None]).astype(jnp.int32), axis=2)
    slot_ids = target_dev * capacity + rank_ids
    own_slot = lax.dynamic_index_in_dim(slot_ids, device, 0, keepdims=False)
    column_ids = jnp.arange(dp_count, dtype=jnp.int32)[:, None] * capacity + rank_ids
    landing = (target_dev == device)[None] & (target_off[None] == row_order[:, None, None])
    source_col = jnp.sum(jnp.where(landing, column_ids[None], 0), axis=(1, 2))
    return (own_slot, source_col)


def pack_rows(source_rows, own_slot, slot_count):
    selector = (jnp.arange(slot_count, dtype=jnp.int32)[:, None] == own_slot[None, :]).astype(
        jnp.bfloat16
    )
    return jnp.dot(selector, source_rows, preferred_element_type=jnp.float32).astype(jnp.bfloat16)


def unpack_rows(arrived, source_col):
    selector = (
        source_col[:, None] == jnp.arange(arrived.shape[0], dtype=jnp.int32)[None, :]
    ).astype(jnp.bfloat16)
    return jnp.dot(selector, arrived, preferred_element_type=jnp.float32).astype(jnp.bfloat16)


def body(resid_in, dest_row, doc_ids, cotangent, gain, steer, w_query, w_keyval, w_out):
    dp_count = lax.axis_size("dp")
    section_count = lax.axis_size("section")
    device = lax.axis_index("dp")
    section_idx = lax.axis_index("section")
    micro_count, row_count, width = resid_in.shape
    capacity = row_count // dp_count + 1
    slot_count = dp_count * capacity
    full_query, full_keyval, full_out = (
        lax.all_gather(w_query[0], "dp", axis=0, tiled=True),
        lax.all_gather(w_keyval[0], "dp", axis=0, tiled=True),
        lax.all_gather(w_out[0], "dp", axis=1, tiled=True),
    )
    gain_row = gain[0]
    steering = steer[0]
    plans = [
        plan_slots(dest_row[micro_idx], device, row_count, capacity, dp_count)
        for micro_idx in range(micro_count)
    ]
    packed = jnp.stack(
        [
            pack_rows(resid_in[micro_idx], plans[micro_idx][0], slot_count).reshape(
                dp_count, capacity, width
            )
            for micro_idx in range(micro_count)
        ],
        axis=1,
    )
    arrived = lax.all_to_all(packed, "dp", split_axis=0, concat_axis=0, tiled=True)
    grouped = jnp.stack(
        [
            unpack_rows(arrived[:, micro_idx].reshape(slot_count, width), plans[micro_idx][1])
            for micro_idx in range(micro_count)
        ]
    )
    global_rows = device * row_count + jnp.arange(row_count, dtype=jnp.int32)
    positions = global_rows[None, :] - doc_ids

    def run_layer(hidden_in, steer_vec):
        return layer(
            hidden_in, steer_vec, gain_row, full_query, full_keyval, full_out, positions, doc_ids
        )

    zero_block = jnp.zeros((micro_count, row_count, width), jnp.bfloat16)
    forward_route = [(i, i + 1) for i in range(section_count - 1)]
    backward_route = [(i + 1, i) for i in range(section_count - 1)]

    def forward_step(carry, step):
        incoming, kept, produced = carry
        active = section_idx == step
        hidden_in = jnp.where(step == 0, grouped, incoming)
        kept = jnp.where(active, hidden_in, kept)
        hidden_new = lax.cond(active, lambda: run_layer(hidden_in, steering), lambda: zero_block)
        produced = jnp.where(active, hidden_new, produced)
        sent = lax.ppermute(hidden_new, "section", forward_route)
        return ((sent, kept, produced), None)

    (unused_in, kept, produced), unused_ys = lax.scan(
        forward_step,
        (zero_block, zero_block, zero_block),
        jnp.arange(section_count, dtype=jnp.int32),
    )

    def backward_step(carry, step):
        incoming, grad_sum = carry
        active = section_idx == step
        upstream = jnp.where(step == section_count - 1, cotangent, incoming)

        def differentiate():
            unused_out, pullback = jax.vjp(run_layer, kept, steering)
            return pullback(upstream)

        grad_in, steer_part = lax.cond(
            active, differentiate, lambda: (zero_block, jnp.zeros_like(steering))
        )
        sent = lax.ppermute(grad_in, "section", backward_route)
        return ((sent, grad_sum + steer_part), None)

    (unused_grad, grad_sum), unused_zs = lax.scan(
        backward_step,
        (zero_block, jnp.zeros_like(steering)),
        jnp.arange(section_count - 1, -1, -1, dtype=jnp.int32),
    )
    total = lax.psum(grad_sum, "dp")
    return (produced[None], total[None])


def solution(mesh):
    in_specs = (
        P(None, "dp", None),
        P(),
        P(None, "dp"),
        P(None, "dp", None),
        P("section", None),
        P("section", None),
        P("section", "dp", None),
        P("section", "dp", None),
        P("section", None, "dp"),
    )
    out_specs = (P("section", None, "dp", None), P("section", None))
    return jax.shard_map(body, mesh=mesh, in_specs=in_specs, out_specs=out_specs, check_vma=False)
```

```python
import jax
import jax.numpy as jnp
from jax import lax
from jax.sharding import PartitionSpec as P

HD = 64


ROPE_BASE = 500000.0
EPSILON = 1e-05
MASKED = -1e30


def rope_tables(positions):
    half_size = HD // 2
    freq_index = jnp.arange(half_size, dtype=jnp.float32)
    inverse = ROPE_BASE ** (-2.0 * freq_index / HD)
    angles = positions.astype(jnp.float32)[..., None] * inverse
    return (jnp.cos(angles)[..., None, :], jnp.sin(angles)[..., None, :])


def rotate(values, tables):
    half_size = values.shape[-1] // 2
    cosine, sine_part = tables
    first_half = values[..., :half_size]
    second = values[..., half_size:]
    return jnp.concatenate(
        [first_half * cosine - second * sine_part, second * cosine + first_half * sine_part],
        axis=-1,
    )


def layer(hidden_in, steering, gain_row, w_qkv, w_out, tables, allowed):
    row_count, width = hidden_in.shape
    head_size = HD
    query_heads = w_out.shape[0] // head_size
    kv_heads = (w_qkv.shape[1] - query_heads * head_size) // (2 * head_size)
    group_size = query_heads // kv_heads
    residual = hidden_in.astype(jnp.float32) + steering
    normed = (
        residual
        * lax.rsqrt(jnp.mean(residual * residual, axis=-1, keepdims=True) + EPSILON)
        * gain_row
    ).astype(jnp.bfloat16)
    projected_in = jnp.dot(normed, w_qkv, preferred_element_type=jnp.float32)
    query_cols = query_heads * head_size
    queries = projected_in[:, :query_cols].reshape(row_count, query_heads, head_size)
    keyval = projected_in[:, query_cols:]
    key_rows = rotate(
        keyval[:, : kv_heads * head_size].reshape(row_count, kv_heads, head_size), tables
    ).astype(jnp.bfloat16)
    values = (
        keyval[:, kv_heads * head_size :]
        .reshape(row_count, kv_heads, head_size)
        .astype(jnp.bfloat16)
    )
    queries = (
        rotate(queries, tables)
        .astype(jnp.bfloat16)
        .reshape(row_count, kv_heads, group_size, head_size)
    )
    scores = jnp.einsum(
        "rkgd,skd->kgrs", queries, key_rows, preferred_element_type=jnp.float32
    ) * head_size ** (-0.5)
    scores = jnp.where(allowed[None, None], scores, MASKED)
    peak = jnp.max(scores, axis=-1, keepdims=True)
    weights = jnp.exp(scores - peak)
    weights = (weights / jnp.sum(weights, axis=-1, keepdims=True)).astype(jnp.bfloat16)
    mixed_heads = jnp.einsum(
        "kgrs,skd->rkgd", weights, values, preferred_element_type=jnp.float32
    ).astype(jnp.bfloat16)
    mixed_heads = mixed_heads.reshape(row_count, query_heads * head_size)
    return (residual + jnp.dot(mixed_heads, w_out, preferred_element_type=jnp.float32)).astype(
        jnp.bfloat16
    )


def butterfly_sum(values, axis):
    count = lax.axis_size(axis)
    distance = 1
    while distance < count:
        route = [(i, i ^ distance) for i in range(count)]
        values = values + lax.ppermute(values, axis, route)
        distance *= 2
    return values


def plan_slots(target, device, row_count, capacity, dp_count):
    target_grid = target.reshape(dp_count, row_count)
    target_dev = target_grid // row_count
    target_off = target_grid % row_count
    row_order = jnp.arange(row_count, dtype=jnp.int32)
    matching = target_dev[:, :, None] == target_dev[:, None, :]
    earlier = row_order[None, :] < row_order[:, None]
    rank_ids = jnp.sum((matching & earlier[None]).astype(jnp.int32), axis=2)
    slot_ids = target_dev * capacity + rank_ids
    own_slot = lax.dynamic_index_in_dim(slot_ids, device, 0, keepdims=False)
    column_ids = jnp.arange(dp_count, dtype=jnp.int32)[:, None] * capacity + rank_ids
    landing = (target_dev == device)[None] & (target_off[None] == row_order[:, None, None])
    source_col = jnp.sum(jnp.where(landing, column_ids[None], 0), axis=(1, 2))
    return (own_slot, source_col)


def pack_rows(source_rows, own_slot, slot_count):
    selector = (jnp.arange(slot_count, dtype=jnp.int32)[:, None] == own_slot[None, :]).astype(
        jnp.bfloat16
    )
    return jnp.dot(selector, source_rows, preferred_element_type=jnp.float32).astype(jnp.bfloat16)


def unpack_rows(arrived, source_col):
    selector = (
        source_col[:, None] == jnp.arange(arrived.shape[0], dtype=jnp.int32)[None, :]
    ).astype(jnp.bfloat16)
    return jnp.dot(selector, arrived, preferred_element_type=jnp.float32).astype(jnp.bfloat16)


def body(resid_in, dest_row, doc_ids, cotangent, gain, steer, w_query, w_keyval, w_out):
    dp_count = lax.axis_size("dp")
    section_count = lax.axis_size("section")
    device = lax.axis_index("dp")
    section_idx = lax.axis_index("section")
    micro_count, row_count, width = resid_in.shape
    capacity = row_count // dp_count + 1
    slot_count = dp_count * capacity
    full_qkv = lax.all_gather(
        jnp.concatenate([w_query[0], w_keyval[0]], axis=1), "dp", axis=0, tiled=True
    )
    full_out = lax.all_gather(w_out[0], "dp", axis=1, tiled=True)
    gain_row = gain[0]
    steering = steer[0]
    plans = [
        plan_slots(dest_row[micro_idx], device, row_count, capacity, dp_count)
        for micro_idx in range(micro_count)
    ]
    packed = jnp.stack(
        [
            pack_rows(resid_in[micro_idx], plans[micro_idx][0], slot_count).reshape(
                dp_count, capacity, width
            )
            for micro_idx in range(micro_count)
        ],
        axis=1,
    )
    arrived = lax.all_to_all(packed, "dp", split_axis=0, concat_axis=0, tiled=True)
    grouped = jnp.stack(
        [
            unpack_rows(arrived[:, micro_idx].reshape(slot_count, width), plans[micro_idx][1])
            for micro_idx in range(micro_count)
        ]
    )
    global_rows = device * row_count + jnp.arange(row_count, dtype=jnp.int32)
    flat_count = micro_count * row_count
    tables = rope_tables((global_rows[None, :] - doc_ids).reshape(flat_count))
    micro_of = jnp.arange(flat_count, dtype=jnp.int32) // row_count
    doc_keys = doc_ids.reshape(flat_count) + micro_of * (dp_count * row_count)
    flat_index = jnp.arange(flat_count, dtype=jnp.int32)
    allowed = (doc_keys[:, None] == doc_keys[None, :]) & (
        flat_index[:, None] >= flat_index[None, :]
    )
    grouped = grouped.reshape(flat_count, width)
    cotangent = cotangent.reshape(flat_count, width)

    def run_layer(hidden_in, steer_vec):
        return layer(hidden_in, steer_vec, gain_row, full_qkv, full_out, tables, allowed)

    zero_block = jnp.zeros((flat_count, width), jnp.bfloat16)
    forward_route = [(i, i + 1) for i in range(section_count - 1)]
    backward_route = [(i + 1, i) for i in range(section_count - 1)]

    def forward_step(carry, step):
        incoming, kept, produced = carry
        active = section_idx == step
        hidden_in = jnp.where(step == 0, grouped, incoming)
        kept = jnp.where(active, hidden_in, kept)
        hidden_new = lax.cond(active, lambda: run_layer(hidden_in, steering), lambda: zero_block)
        produced = jnp.where(active, hidden_new, produced)
        sent = lax.ppermute(hidden_new, "section", forward_route)
        return ((sent, kept, produced), None)

    (unused_in, kept, produced), unused_ys = lax.scan(
        forward_step,
        (zero_block, zero_block, zero_block),
        jnp.arange(section_count, dtype=jnp.int32),
    )

    def backward_step(carry, step):
        incoming, grad_sum = carry
        active = section_idx == step
        upstream = jnp.where(step == section_count - 1, cotangent, incoming)

        def differentiate():
            unused_out, pullback = jax.vjp(run_layer, kept, steering)
            return pullback(upstream)

        grad_in, steer_part = lax.cond(
            active, differentiate, lambda: (zero_block, jnp.zeros_like(steering))
        )
        sent = lax.ppermute(grad_in, "section", backward_route)
        return ((sent, grad_sum + steer_part), None)

    (unused_grad, grad_sum), unused_zs = lax.scan(
        backward_step,
        (zero_block, jnp.zeros_like(steering)),
        jnp.arange(section_count - 1, -1, -1, dtype=jnp.int32),
    )
    total = butterfly_sum(grad_sum, "dp")
    return (produced.reshape(1, micro_count, row_count, width), total[None])


def solution(mesh):
    in_specs = (
        P(None, "dp", None),
        P(),
        P(None, "dp"),
        P(None, "dp", None),
        P("section", None),
        P("section", None),
        P("section", "dp", None),
        P("section", "dp", None),
        P("section", None, "dp"),
    )
    out_specs = (P("section", None, "dp", None), P("section", None))
    return jax.shard_map(body, mesh=mesh, in_specs=in_specs, out_specs=out_specs, check_vma=False)
```

```python
import jax
import jax.numpy as jnp
from jax import lax
from jax.sharding import PartitionSpec as P

HD = 64


ROPE_BASE = 500000.0
EPSILON = 1e-05
MASKED = -1e30


def rope_tables(positions):
    half_size = HD // 2
    freq_index = jnp.arange(half_size, dtype=jnp.float32)
    inverse = ROPE_BASE ** (-2.0 * freq_index / HD)
    angles = positions.astype(jnp.float32)[..., None] * inverse
    return (jnp.cos(angles)[..., None, :], jnp.sin(angles)[..., None, :])


def rotate(values, tables):
    half_size = values.shape[-1] // 2
    cosine, sine_part = tables
    first_half = values[..., :half_size]
    second = values[..., half_size:]
    return jnp.concatenate(
        [first_half * cosine - second * sine_part, second * cosine + first_half * sine_part],
        axis=-1,
    )


def layer(hidden_in, steering, gain_row, w_qkv, w_out_t, tables, allowed):
    row_count, width = hidden_in.shape
    head_size = HD
    query_heads = w_out_t.shape[1] // head_size
    kv_heads = (w_qkv.shape[1] - query_heads * head_size) // (2 * head_size)
    group_size = query_heads // kv_heads
    residual = hidden_in.astype(jnp.float32) + steering
    normed = (
        residual
        * lax.rsqrt(jnp.mean(residual * residual, axis=-1, keepdims=True) + EPSILON)
        * gain_row
    ).astype(jnp.bfloat16)
    projected_in = jnp.dot(normed, w_qkv, preferred_element_type=jnp.float32)
    query_cols = query_heads * head_size
    queries = projected_in[:, :query_cols].reshape(row_count, query_heads, head_size)
    keyval = projected_in[:, query_cols:]
    key_rows = rotate(
        keyval[:, : kv_heads * head_size].reshape(row_count, kv_heads, head_size), tables
    ).astype(jnp.bfloat16)
    values = (
        keyval[:, kv_heads * head_size :]
        .reshape(row_count, kv_heads, head_size)
        .astype(jnp.bfloat16)
    )
    queries = (
        rotate(queries, tables)
        .astype(jnp.bfloat16)
        .reshape(row_count, kv_heads, group_size, head_size)
    )
    scores = jnp.einsum(
        "rkgd,skd->kgrs", queries, key_rows, preferred_element_type=jnp.float32
    ) * head_size ** (-0.5)
    scores = jnp.where(allowed[None, None], scores, MASKED)
    peak = jnp.max(scores, axis=-1, keepdims=True)
    weights = jnp.exp(scores - peak)
    weights = (weights / jnp.sum(weights, axis=-1, keepdims=True)).astype(jnp.bfloat16)
    mixed_heads = jnp.einsum(
        "kgrs,skd->rkgd", weights, values, preferred_element_type=jnp.float32
    ).astype(jnp.bfloat16)
    mixed_heads = mixed_heads.reshape(row_count, query_heads * head_size)
    projected = lax.dot_general(
        mixed_heads, w_out_t, (((1,), (1,)), ((), ())), preferred_element_type=jnp.float32
    )
    return (residual + projected).astype(jnp.bfloat16)


def butterfly_sum(values, axis):
    count = lax.axis_size(axis)
    distance = 1
    while distance < count:
        route = [(i, i ^ distance) for i in range(count)]
        values = values + lax.ppermute(values, axis, route)
        distance *= 2
    return values


def plan_slots(target, device, row_count, capacity, dp_count):
    target_grid = target.reshape(dp_count, row_count)
    target_dev = target_grid // row_count
    target_off = target_grid % row_count
    row_order = jnp.arange(row_count, dtype=jnp.int32)
    matching = target_dev[:, :, None] == target_dev[:, None, :]
    earlier = row_order[None, :] < row_order[:, None]
    rank_ids = jnp.sum((matching & earlier[None]).astype(jnp.int32), axis=2)
    slot_ids = target_dev * capacity + rank_ids
    own_slot = lax.dynamic_index_in_dim(slot_ids, device, 0, keepdims=False)
    column_ids = jnp.arange(dp_count, dtype=jnp.int32)[:, None] * capacity + rank_ids
    landing = (target_dev == device)[None] & (target_off[None] == row_order[:, None, None])
    source_col = jnp.sum(jnp.where(landing, column_ids[None], 0), axis=(1, 2))
    return (own_slot, source_col)


def pack_rows(source_rows, own_slot, slot_count):
    selector = (jnp.arange(slot_count, dtype=jnp.int32)[:, None] == own_slot[None, :]).astype(
        jnp.bfloat16
    )
    return jnp.dot(selector, source_rows, preferred_element_type=jnp.float32).astype(jnp.bfloat16)


def unpack_rows(arrived, source_col):
    selector = (
        source_col[:, None] == jnp.arange(arrived.shape[0], dtype=jnp.int32)[None, :]
    ).astype(jnp.bfloat16)
    return jnp.dot(selector, arrived, preferred_element_type=jnp.float32).astype(jnp.bfloat16)


def body(resid_in, dest_row, doc_ids, cotangent, gain, steer, w_query, w_keyval, w_out):
    dp_count = lax.axis_size("dp")
    section_count = lax.axis_size("section")
    device = lax.axis_index("dp")
    section_idx = lax.axis_index("section")
    micro_count, row_count, width = resid_in.shape
    capacity = row_count // dp_count + 1
    slot_count = dp_count * capacity
    qkv_cols = w_query.shape[2] + w_keyval.shape[2]
    full_slab = lax.all_gather(
        jnp.concatenate([w_query[0], w_keyval[0], w_out[0].T], axis=1), "dp", axis=0, tiled=True
    )
    full_qkv = full_slab[:, :qkv_cols]
    full_out_t = full_slab[:, qkv_cols:]
    gain_row = gain[0]
    steering = steer[0]
    plans = [
        plan_slots(dest_row[micro_idx], device, row_count, capacity, dp_count)
        for micro_idx in range(micro_count)
    ]
    packed = jnp.stack(
        [
            pack_rows(resid_in[micro_idx], plans[micro_idx][0], slot_count).reshape(
                dp_count, capacity, width
            )
            for micro_idx in range(micro_count)
        ],
        axis=1,
    )
    arrived = lax.all_to_all(packed, "dp", split_axis=0, concat_axis=0, tiled=True)
    grouped = jnp.stack(
        [
            unpack_rows(arrived[:, micro_idx].reshape(slot_count, width), plans[micro_idx][1])
            for micro_idx in range(micro_count)
        ]
    )
    global_rows = device * row_count + jnp.arange(row_count, dtype=jnp.int32)
    flat_count = micro_count * row_count
    tables = rope_tables((global_rows[None, :] - doc_ids).reshape(flat_count))
    micro_of = jnp.arange(flat_count, dtype=jnp.int32) // row_count
    doc_keys = doc_ids.reshape(flat_count) + micro_of * (dp_count * row_count)
    flat_index = jnp.arange(flat_count, dtype=jnp.int32)
    allowed = (doc_keys[:, None] == doc_keys[None, :]) & (
        flat_index[:, None] >= flat_index[None, :]
    )
    grouped = grouped.reshape(flat_count, width)
    cotangent = cotangent.reshape(flat_count, width)

    def run_layer(hidden_in, steer_vec):
        return layer(hidden_in, steer_vec, gain_row, full_qkv, full_out_t, tables, allowed)

    zero_block = jnp.zeros((flat_count, width), jnp.bfloat16)
    forward_route = [(i, i + 1) for i in range(section_count - 1)]
    backward_route = [(i + 1, i) for i in range(section_count - 1)]

    def forward_step(carry, step):
        incoming, kept, produced = carry
        active = section_idx == step
        hidden_in = jnp.where(step == 0, grouped, incoming)
        kept = jnp.where(active, hidden_in, kept)
        hidden_new = lax.cond(active, lambda: run_layer(hidden_in, steering), lambda: zero_block)
        produced = jnp.where(active, hidden_new, produced)
        sent = lax.ppermute(hidden_new, "section", forward_route)
        return ((sent, kept, produced), None)

    (unused_in, kept, produced), unused_ys = lax.scan(
        forward_step,
        (zero_block, zero_block, zero_block),
        jnp.arange(section_count, dtype=jnp.int32),
    )

    def backward_step(carry, step):
        incoming, grad_sum = carry
        active = section_idx == step
        upstream = jnp.where(step == section_count - 1, cotangent, incoming)

        def differentiate():
            unused_out, pullback = jax.vjp(run_layer, kept, steering)
            return pullback(upstream)

        grad_in, steer_part = lax.cond(
            active, differentiate, lambda: (zero_block, jnp.zeros_like(steering))
        )
        sent = lax.ppermute(grad_in, "section", backward_route)
        return ((sent, grad_sum + steer_part), None)

    (unused_grad, grad_sum), unused_zs = lax.scan(
        backward_step,
        (zero_block, jnp.zeros_like(steering)),
        jnp.arange(section_count - 1, -1, -1, dtype=jnp.int32),
    )
    total = butterfly_sum(grad_sum, "dp")
    return (produced.reshape(1, micro_count, row_count, width), total[None])


def solution(mesh):
    in_specs = (
        P(None, "dp", None),
        P(),
        P(None, "dp"),
        P(None, "dp", None),
        P("section", None),
        P("section", None),
        P("section", "dp", None),
        P("section", "dp", None),
        P("section", None, "dp"),
    )
    out_specs = (P("section", None, "dp", None), P("section", None))
    return jax.shard_map(body, mesh=mesh, in_specs=in_specs, out_specs=out_specs, check_vma=False)
```

```python
import jax
import jax.numpy as jnp
from jax import lax
from jax.sharding import PartitionSpec as P

HD = 64


ROPE_BASE = 500000.0
EPSILON = 1e-05
MASKED = -1e30


def rope_tables(positions):
    half_size = HD // 2
    freq_index = jnp.arange(half_size, dtype=jnp.float32)
    inverse = ROPE_BASE ** (-2.0 * freq_index / HD)
    angles = positions.astype(jnp.float32)[..., None] * inverse
    return (jnp.cos(angles)[..., None, :], jnp.sin(angles)[..., None, :])


def rotate(values, tables):
    half_size = values.shape[-1] // 2
    cosine, sine_part = tables
    first_half = values[..., :half_size]
    second = values[..., half_size:]
    return jnp.concatenate(
        [first_half * cosine - second * sine_part, second * cosine + first_half * sine_part],
        axis=-1,
    )


def layer(hidden_in, steering, gain_row, w_qkv, w_out, tables, allowed):
    row_count, width = hidden_in.shape
    head_size = HD
    query_heads = w_out.shape[0] // head_size
    kv_heads = (w_qkv.shape[1] - query_heads * head_size) // (2 * head_size)
    group_size = query_heads // kv_heads
    residual = hidden_in.astype(jnp.float32) + steering
    normed = (
        residual
        * lax.rsqrt(jnp.mean(residual * residual, axis=-1, keepdims=True) + EPSILON)
        * gain_row
    ).astype(jnp.bfloat16)
    projected_in = jnp.dot(normed, w_qkv, preferred_element_type=jnp.float32)
    query_cols = query_heads * head_size
    queries = projected_in[:, :query_cols].reshape(row_count, query_heads, head_size)
    keyval = projected_in[:, query_cols:]
    key_rows = rotate(
        keyval[:, : kv_heads * head_size].reshape(row_count, kv_heads, head_size), tables
    ).astype(jnp.bfloat16)
    values = (
        keyval[:, kv_heads * head_size :]
        .reshape(row_count, kv_heads, head_size)
        .astype(jnp.bfloat16)
    )
    queries = (
        rotate(queries, tables)
        .astype(jnp.bfloat16)
        .reshape(row_count, kv_heads, group_size, head_size)
    )
    scores = jnp.einsum(
        "rkgd,skd->kgrs", queries, key_rows, preferred_element_type=jnp.float32
    ) * head_size ** (-0.5)
    scores = jnp.where(allowed[None, None], scores, MASKED)
    peak = jnp.max(scores, axis=-1, keepdims=True)
    weights = jnp.exp(scores - peak)
    weights = (weights / jnp.sum(weights, axis=-1, keepdims=True)).astype(jnp.bfloat16)
    mixed_heads = jnp.einsum(
        "kgrs,skd->rkgd", weights, values, preferred_element_type=jnp.float32
    ).astype(jnp.bfloat16)
    mixed_heads = mixed_heads.reshape(row_count, query_heads * head_size)
    return (residual + jnp.dot(mixed_heads, w_out, preferred_element_type=jnp.float32)).astype(
        jnp.bfloat16
    )


def butterfly_sum(values, axis):
    count = lax.axis_size(axis)
    distance = 1
    while distance < count:
        route = [(i, i ^ distance) for i in range(count)]
        values = values + lax.ppermute(values, axis, route)
        distance *= 2
    return values


def plan_slots(target, device, row_count, capacity, dp_count):
    target_grid = target.reshape(dp_count, row_count)
    target_dev = target_grid // row_count
    target_off = target_grid % row_count
    row_order = jnp.arange(row_count, dtype=jnp.int32)
    matching = target_dev[:, :, None] == target_dev[:, None, :]
    earlier = row_order[None, :] < row_order[:, None]
    rank_ids = jnp.sum((matching & earlier[None]).astype(jnp.int32), axis=2)
    slot_ids = target_dev * capacity + rank_ids
    own_slot = lax.dynamic_index_in_dim(slot_ids, device, 0, keepdims=False)
    column_ids = jnp.arange(dp_count, dtype=jnp.int32)[:, None] * capacity + rank_ids
    landing = (target_dev == device)[None] & (target_off[None] == row_order[:, None, None])
    source_col = jnp.sum(jnp.where(landing, column_ids[None], 0), axis=(1, 2))
    return (own_slot, source_col)


def pack_rows(source_rows, own_slot, slot_count):
    selector = (jnp.arange(slot_count, dtype=jnp.int32)[:, None] == own_slot[None, :]).astype(
        jnp.bfloat16
    )
    return jnp.dot(selector, source_rows, preferred_element_type=jnp.float32).astype(jnp.bfloat16)


def unpack_rows(arrived, source_col):
    selector = (
        source_col[:, None] == jnp.arange(arrived.shape[0], dtype=jnp.int32)[None, :]
    ).astype(jnp.bfloat16)
    return jnp.dot(selector, arrived, preferred_element_type=jnp.float32).astype(jnp.bfloat16)


def body(resid_in, dest_row, doc_ids, cotangent, gain, steer, w_query, w_keyval, w_out):
    dp_count = lax.axis_size("dp")
    section_count = lax.axis_size("section")
    device = lax.axis_index("dp")
    section_idx = lax.axis_index("section")
    micro_count, row_count, width = resid_in.shape
    capacity = row_count // dp_count + 1
    slot_count = dp_count * capacity
    qkv_cols = w_query.shape[2] + w_keyval.shape[2]
    full_slab = lax.all_gather(
        jnp.concatenate([w_query[0], w_keyval[0], w_out[0].T], axis=1), "dp", axis=0, tiled=True
    )
    full_qkv, full_out = lax.optimization_barrier(
        (full_slab[:, :qkv_cols], full_slab[:, qkv_cols:].T)
    )
    gain_row = gain[0]
    steering = steer[0]
    plans = [
        plan_slots(dest_row[micro_idx], device, row_count, capacity, dp_count)
        for micro_idx in range(micro_count)
    ]
    packed = jnp.stack(
        [
            pack_rows(resid_in[micro_idx], plans[micro_idx][0], slot_count).reshape(
                dp_count, capacity, width
            )
            for micro_idx in range(micro_count)
        ],
        axis=1,
    )
    arrived = lax.all_to_all(packed, "dp", split_axis=0, concat_axis=0, tiled=True)
    grouped = jnp.stack(
        [
            unpack_rows(arrived[:, micro_idx].reshape(slot_count, width), plans[micro_idx][1])
            for micro_idx in range(micro_count)
        ]
    )
    global_rows = device * row_count + jnp.arange(row_count, dtype=jnp.int32)
    flat_count = micro_count * row_count
    tables = rope_tables((global_rows[None, :] - doc_ids).reshape(flat_count))
    micro_of = jnp.arange(flat_count, dtype=jnp.int32) // row_count
    doc_keys = doc_ids.reshape(flat_count) + micro_of * (dp_count * row_count)
    flat_index = jnp.arange(flat_count, dtype=jnp.int32)
    allowed = (doc_keys[:, None] == doc_keys[None, :]) & (
        flat_index[:, None] >= flat_index[None, :]
    )
    grouped = grouped.reshape(flat_count, width)
    cotangent = cotangent.reshape(flat_count, width)

    def run_layer(hidden_in, steer_vec):
        return layer(hidden_in, steer_vec, gain_row, full_qkv, full_out, tables, allowed)

    zero_block = jnp.zeros((flat_count, width), jnp.bfloat16)
    forward_route = [(i, i + 1) for i in range(section_count - 1)]
    backward_route = [(i + 1, i) for i in range(section_count - 1)]

    def forward_step(carry, step):
        incoming, kept, produced = carry
        active = section_idx == step
        hidden_in = jnp.where(step == 0, grouped, incoming)
        kept = jnp.where(active, hidden_in, kept)
        hidden_new = lax.cond(active, lambda: run_layer(hidden_in, steering), lambda: zero_block)
        produced = jnp.where(active, hidden_new, produced)
        sent = lax.ppermute(hidden_new, "section", forward_route)
        return ((sent, kept, produced), None)

    (unused_in, kept, produced), unused_ys = lax.scan(
        forward_step,
        (zero_block, zero_block, zero_block),
        jnp.arange(section_count, dtype=jnp.int32),
    )

    def backward_step(carry, step):
        incoming, grad_sum = carry
        active = section_idx == step
        upstream = jnp.where(step == section_count - 1, cotangent, incoming)

        def differentiate():
            unused_out, pullback = jax.vjp(run_layer, kept, steering)
            return pullback(upstream)

        grad_in, steer_part = lax.cond(
            active, differentiate, lambda: (zero_block, jnp.zeros_like(steering))
        )
        sent = lax.ppermute(grad_in, "section", backward_route)
        return ((sent, grad_sum + steer_part), None)

    (unused_grad, grad_sum), unused_zs = lax.scan(
        backward_step,
        (zero_block, jnp.zeros_like(steering)),
        jnp.arange(section_count - 1, -1, -1, dtype=jnp.int32),
    )
    total = butterfly_sum(grad_sum, "dp")
    return (produced.reshape(1, micro_count, row_count, width), total[None])


def solution(mesh):
    in_specs = (
        P(None, "dp", None),
        P(),
        P(None, "dp"),
        P(None, "dp", None),
        P("section", None),
        P("section", None),
        P("section", "dp", None),
        P("section", "dp", None),
        P("section", None, "dp"),
    )
    out_specs = (P("section", None, "dp", None), P("section", None))
    return jax.shard_map(body, mesh=mesh, in_specs=in_specs, out_specs=out_specs, check_vma=False)
```

```python
import jax
import jax.numpy as jnp
from jax import lax
from jax.sharding import PartitionSpec as P

HD = 64


ROPE_BASE = 500000.0
EPSILON = 1e-05
MASKED = -1e30


def rope_tables(positions):
    half_size = HD // 2
    freq_index = jnp.arange(half_size, dtype=jnp.float32)
    inverse = ROPE_BASE ** (-2.0 * freq_index / HD)
    angles = positions.astype(jnp.float32)[..., None] * inverse
    return (jnp.cos(angles)[..., None, :], jnp.sin(angles)[..., None, :])


def rotate(values, tables):
    half_size = values.shape[-1] // 2
    cosine, sine_part = tables
    first_half = values[..., :half_size]
    second = values[..., half_size:]
    return jnp.concatenate(
        [first_half * cosine - second * sine_part, second * cosine + first_half * sine_part],
        axis=-1,
    )


def layer(hidden_in, steering, gain_row, w_qkv, w_out, tables, allowed):
    row_count, width = hidden_in.shape
    head_size = HD
    query_heads = w_out.shape[0] // head_size
    kv_heads = (w_qkv.shape[1] - query_heads * head_size) // (2 * head_size)
    group_size = query_heads // kv_heads
    residual = hidden_in.astype(jnp.float32) + steering
    normed = (
        residual
        * lax.rsqrt(jnp.mean(residual * residual, axis=-1, keepdims=True) + EPSILON)
        * gain_row
    ).astype(jnp.bfloat16)
    projected_in = jnp.dot(normed, w_qkv, preferred_element_type=jnp.float32)
    query_cols = query_heads * head_size
    queries = projected_in[:, :query_cols].reshape(row_count, query_heads, head_size)
    keyval = projected_in[:, query_cols:]
    key_rows = rotate(
        keyval[:, : kv_heads * head_size].reshape(row_count, kv_heads, head_size), tables
    ).astype(jnp.bfloat16)
    values = (
        keyval[:, kv_heads * head_size :]
        .reshape(row_count, kv_heads, head_size)
        .astype(jnp.bfloat16)
    )
    queries = (
        rotate(queries, tables)
        .astype(jnp.bfloat16)
        .reshape(row_count, kv_heads, group_size, head_size)
    )
    scores = jnp.einsum(
        "rkgd,skd->kgrs", queries, key_rows, preferred_element_type=jnp.float32
    ) * head_size ** (-0.5)
    scores = jnp.where(allowed[None, None], scores, MASKED)
    peak = jnp.max(scores, axis=-1, keepdims=True)
    weights = jnp.exp(scores - peak)
    weights = (weights / jnp.sum(weights, axis=-1, keepdims=True)).astype(jnp.bfloat16)
    mixed_heads = jnp.einsum(
        "kgrs,skd->rkgd", weights, values, preferred_element_type=jnp.float32
    ).astype(jnp.bfloat16)
    mixed_heads = mixed_heads.reshape(row_count, query_heads * head_size)
    return (residual + jnp.dot(mixed_heads, w_out, preferred_element_type=jnp.float32)).astype(
        jnp.bfloat16
    )


def butterfly_sum(values, axis):
    count = lax.axis_size(axis)
    distance = 1
    while distance < count:
        route = [(i, i ^ distance) for i in range(count)]
        values = values + lax.ppermute(values, axis, route)
        distance *= 2
    return values


def plan_slots(target, device, row_count, capacity, dp_count):
    target_grid = target.reshape(dp_count, row_count)
    target_dev = target_grid // row_count
    target_off = target_grid % row_count
    row_order = jnp.arange(row_count, dtype=jnp.int32)
    matching = target_dev[:, :, None] == target_dev[:, None, :]
    earlier = row_order[None, :] < row_order[:, None]
    rank_ids = jnp.sum((matching & earlier[None]).astype(jnp.int32), axis=2)
    slot_ids = target_dev * capacity + rank_ids
    own_slot = lax.dynamic_index_in_dim(slot_ids, device, 0, keepdims=False)
    column_ids = jnp.arange(dp_count, dtype=jnp.int32)[:, None] * capacity + rank_ids
    landing = (target_dev == device)[None] & (target_off[None] == row_order[:, None, None])
    source_col = jnp.sum(jnp.where(landing, column_ids[None], 0), axis=(1, 2))
    return (own_slot, source_col)


def pack_rows(source_rows, own_slot, slot_count):
    selector = (jnp.arange(slot_count, dtype=jnp.int32)[:, None] == own_slot[None, :]).astype(
        jnp.bfloat16
    )
    return jnp.dot(selector, source_rows, preferred_element_type=jnp.float32).astype(jnp.bfloat16)


def unpack_rows(arrived, source_col):
    selector = (
        source_col[:, None] == jnp.arange(arrived.shape[0], dtype=jnp.int32)[None, :]
    ).astype(jnp.bfloat16)
    return jnp.dot(selector, arrived, preferred_element_type=jnp.float32).astype(jnp.bfloat16)


def body(resid_in, dest_row, doc_ids, cotangent, gain, steer, w_query, w_keyval, w_out):
    dp_count = lax.axis_size("dp")
    section_count = lax.axis_size("section")
    device = lax.axis_index("dp")
    section_idx = lax.axis_index("section")
    micro_count, row_count, width = resid_in.shape
    capacity = row_count // dp_count + 1
    slot_count = dp_count * capacity
    full_qkv = lax.all_gather(
        jnp.concatenate([w_query[0], w_keyval[0]], axis=1), "dp", axis=0, tiled=True
    )
    full_out = lax.all_gather(w_out[0], "dp", axis=1, tiled=True)
    gain_row = gain[0]
    steering = steer[0]
    plans = [
        plan_slots(dest_row[micro_idx], device, row_count, capacity, dp_count)
        for micro_idx in range(micro_count)
    ]
    packed = jnp.stack(
        [
            pack_rows(resid_in[micro_idx], plans[micro_idx][0], slot_count).reshape(
                dp_count, capacity, width
            )
            for micro_idx in range(micro_count)
        ],
        axis=1,
    )
    arrived = lax.all_to_all(packed, "dp", split_axis=0, concat_axis=0, tiled=True)
    grouped = jnp.stack(
        [
            unpack_rows(arrived[:, micro_idx].reshape(slot_count, width), plans[micro_idx][1])
            for micro_idx in range(micro_count)
        ]
    )
    global_rows = device * row_count + jnp.arange(row_count, dtype=jnp.int32)
    flat_count = micro_count * row_count
    tables = rope_tables((global_rows[None, :] - doc_ids).reshape(flat_count))
    micro_of = jnp.arange(flat_count, dtype=jnp.int32) // row_count
    doc_keys = doc_ids.reshape(flat_count) + micro_of * (dp_count * row_count)
    flat_index = jnp.arange(flat_count, dtype=jnp.int32)
    allowed = (doc_keys[:, None] == doc_keys[None, :]) & (
        flat_index[:, None] >= flat_index[None, :]
    )
    grouped = grouped.reshape(flat_count, width)
    cotangent = cotangent.reshape(flat_count, width)

    def run_layer(hidden_in, steer_vec):
        return layer(hidden_in, steer_vec, gain_row, full_qkv, full_out, tables, allowed)

    zero_block = jnp.zeros((flat_count, width), jnp.bfloat16)
    forward_route = [(i, i + 1) for i in range(section_count - 1)]
    backward_route = [(i + 1, i) for i in range(section_count - 1)]

    def forward_step(carry, unused):
        hidden_in, kept, produced, step = carry
        active = section_idx == step
        kept = jnp.where(active, hidden_in, kept)
        hidden_new = lax.cond(active, lambda: run_layer(hidden_in, steering), lambda: zero_block)
        produced = jnp.where(active, hidden_new, produced)
        sent = lax.ppermute(hidden_new, "section", forward_route)
        return ((sent, kept, produced, step + 1), None)

    (unused_in, kept, produced, unused_step), unused_ys = lax.scan(
        forward_step, (grouped, zero_block, zero_block, jnp.int32(0)), None, length=section_count
    )

    def backward_step(carry, unused):
        upstream, grad_sum, step = carry
        active = section_idx == step

        def differentiate():
            unused_out, pullback = jax.vjp(run_layer, kept, steering)
            return pullback(upstream)

        grad_in, steer_part = lax.cond(
            active, differentiate, lambda: (zero_block, jnp.zeros_like(steering))
        )
        sent = lax.ppermute(grad_in, "section", backward_route)
        return ((sent, grad_sum + steer_part, step - 1), None)

    (unused_grad, grad_sum, unused_step), unused_zs = lax.scan(
        backward_step,
        (cotangent, jnp.zeros_like(steering), jnp.int32(section_count - 1)),
        None,
        length=section_count,
    )

    total = butterfly_sum(grad_sum, "dp")
    return (produced.reshape(1, micro_count, row_count, width), total[None])


def solution(mesh):
    in_specs = (
        P(None, "dp", None),
        P(),
        P(None, "dp"),
        P(None, "dp", None),
        P("section", None),
        P("section", None),
        P("section", "dp", None),
        P("section", "dp", None),
        P("section", None, "dp"),
    )
    out_specs = (P("section", None, "dp", None), P("section", None))
    return jax.shard_map(body, mesh=mesh, in_specs=in_specs, out_specs=out_specs, check_vma=False)
```

```python
import jax
import jax.numpy as jnp
from jax import lax
from jax.sharding import PartitionSpec as P

HD = 64


ROPE_BASE = 500000.0
EPSILON = 1e-05
MASKED = -1e30


def rope_tables(positions):
    half_size = HD // 2
    freq_index = jnp.arange(half_size, dtype=jnp.float32)
    inverse = ROPE_BASE ** (-2.0 * freq_index / HD)
    angles = positions.astype(jnp.float32)[..., None] * inverse
    return (jnp.cos(angles)[..., None, :], jnp.sin(angles)[..., None, :])


def rotate(values, tables):
    half_size = values.shape[-1] // 2
    cosine, sine_part = tables
    first_half = values[..., :half_size]
    second = values[..., half_size:]
    return jnp.concatenate(
        [first_half * cosine - second * sine_part, second * cosine + first_half * sine_part],
        axis=-1,
    )


def normalize(hidden_in, steering, gain_row):
    residual = hidden_in.astype(jnp.float32) + steering
    normed = (
        residual
        * lax.rsqrt(jnp.mean(residual * residual, axis=-1, keepdims=True) + EPSILON)
        * gain_row
    ).astype(jnp.bfloat16)
    return (residual, normed)


def attend(projected_in, tables, allowed, query_heads):
    row_count = projected_in.shape[0]
    head_size = HD
    query_cols = query_heads * head_size
    kv_heads = (projected_in.shape[1] - query_cols) // (2 * head_size)
    group_size = query_heads // kv_heads
    queries = projected_in[:, :query_cols].reshape(row_count, query_heads, head_size)
    keyval = projected_in[:, query_cols:]
    key_rows = rotate(
        keyval[:, : kv_heads * head_size].reshape(row_count, kv_heads, head_size), tables
    ).astype(jnp.bfloat16)
    values = (
        keyval[:, kv_heads * head_size :]
        .reshape(row_count, kv_heads, head_size)
        .astype(jnp.bfloat16)
    )
    queries = (
        rotate(queries, tables)
        .astype(jnp.bfloat16)
        .reshape(row_count, kv_heads, group_size, head_size)
    )
    scores = jnp.einsum(
        "rkgd,skd->kgrs", queries, key_rows, preferred_element_type=jnp.float32
    ) * head_size ** (-0.5)
    scores = jnp.where(allowed[None, None], scores, MASKED)
    peak = jnp.max(scores, axis=-1, keepdims=True)
    weights = jnp.exp(scores - peak)
    weights = (weights / jnp.sum(weights, axis=-1, keepdims=True)).astype(jnp.bfloat16)
    mixed_heads = jnp.einsum(
        "kgrs,skd->rkgd", weights, values, preferred_element_type=jnp.float32
    ).astype(jnp.bfloat16)
    return mixed_heads.reshape(row_count, query_heads * head_size)


def project_in(normed, w_qkv):
    return jnp.dot(normed, w_qkv, preferred_element_type=jnp.float32)


def project_out(residual, mixed_heads, w_out):
    return (residual + jnp.dot(mixed_heads, w_out, preferred_element_type=jnp.float32)).astype(
        jnp.bfloat16
    )


def layer_forward(hidden_in, steering, gain_row, w_qkv, w_out, tables, allowed):
    residual, normed = normalize(hidden_in, steering, gain_row)
    projected_in = project_in(normed, w_qkv)
    mixed_heads = attend(projected_in, tables, allowed, w_out.shape[0] // HD)
    return (project_out(residual, mixed_heads, w_out), projected_in)


def layer_backward(
    hidden_in, steering, projected_in, upstream, gain_row, w_qkv, w_out, tables, allowed
):
    query_heads = w_out.shape[0] // HD
    (residual, normed), normalize_pull = jax.vjp(
        lambda h, s: normalize(h, s, gain_row), hidden_in, steering
    )
    mixed_heads, attend_pull = jax.vjp(
        lambda p: attend(p, tables, allowed, query_heads), projected_in
    )
    unused_out, out_pull = jax.vjp(
        lambda r, m: project_out(r, m, w_out), residual, mixed_heads
    )
    grad_residual, grad_mixed = out_pull(upstream)
    (grad_projected,) = attend_pull(grad_mixed)
    unused_proj, in_pull = jax.vjp(lambda n: project_in(n, w_qkv), normed)
    (grad_normed,) = in_pull(grad_projected)
    return normalize_pull((grad_residual, grad_normed))


def butterfly_sum(values, axis):
    count = lax.axis_size(axis)
    distance = 1
    while distance < count:
        route = [(i, i ^ distance) for i in range(count)]
        values = values + lax.ppermute(values, axis, route)
        distance *= 2
    return values


def plan_slots(target, device, row_count, capacity, dp_count):
    target_grid = target.reshape(dp_count, row_count)
    target_dev = target_grid // row_count
    target_off = target_grid % row_count
    row_order = jnp.arange(row_count, dtype=jnp.int32)
    matching = target_dev[:, :, None] == target_dev[:, None, :]
    earlier = row_order[None, :] < row_order[:, None]
    rank_ids = jnp.sum((matching & earlier[None]).astype(jnp.int32), axis=2)
    slot_ids = target_dev * capacity + rank_ids
    own_slot = lax.dynamic_index_in_dim(slot_ids, device, 0, keepdims=False)
    column_ids = jnp.arange(dp_count, dtype=jnp.int32)[:, None] * capacity + rank_ids
    landing = (target_dev == device)[None] & (target_off[None] == row_order[:, None, None])
    source_col = jnp.sum(jnp.where(landing, column_ids[None], 0), axis=(1, 2))
    return (own_slot, source_col)


def pack_rows(source_rows, own_slot, slot_count):
    selector = (jnp.arange(slot_count, dtype=jnp.int32)[:, None] == own_slot[None, :]).astype(
        jnp.bfloat16
    )
    return jnp.dot(selector, source_rows, preferred_element_type=jnp.float32).astype(jnp.bfloat16)


def unpack_rows(arrived, source_col):
    selector = (
        source_col[:, None] == jnp.arange(arrived.shape[0], dtype=jnp.int32)[None, :]
    ).astype(jnp.bfloat16)
    return jnp.dot(selector, arrived, preferred_element_type=jnp.float32).astype(jnp.bfloat16)


def body(resid_in, dest_row, doc_ids, cotangent, gain, steer, w_query, w_keyval, w_out):
    dp_count = lax.axis_size("dp")
    section_count = lax.axis_size("section")
    device = lax.axis_index("dp")
    section_idx = lax.axis_index("section")
    micro_count, row_count, width = resid_in.shape
    capacity = row_count // dp_count + 1
    slot_count = dp_count * capacity
    full_qkv = lax.all_gather(
        jnp.concatenate([w_query[0], w_keyval[0]], axis=1), "dp", axis=0, tiled=True
    )
    full_out = lax.all_gather(w_out[0], "dp", axis=1, tiled=True)
    gain_row = gain[0]
    steering = steer[0]
    plans = [
        plan_slots(dest_row[micro_idx], device, row_count, capacity, dp_count)
        for micro_idx in range(micro_count)
    ]
    packed = jnp.stack(
        [
            pack_rows(resid_in[micro_idx], plans[micro_idx][0], slot_count).reshape(
                dp_count, capacity, width
            )
            for micro_idx in range(micro_count)
        ],
        axis=1,
    )
    arrived = lax.all_to_all(packed, "dp", split_axis=0, concat_axis=0, tiled=True)
    grouped = jnp.stack(
        [
            unpack_rows(arrived[:, micro_idx].reshape(slot_count, width), plans[micro_idx][1])
            for micro_idx in range(micro_count)
        ]
    )
    global_rows = device * row_count + jnp.arange(row_count, dtype=jnp.int32)
    flat_count = micro_count * row_count
    tables = rope_tables((global_rows[None, :] - doc_ids).reshape(flat_count))
    micro_of = jnp.arange(flat_count, dtype=jnp.int32) // row_count
    doc_keys = doc_ids.reshape(flat_count) + micro_of * (dp_count * row_count)
    flat_index = jnp.arange(flat_count, dtype=jnp.int32)
    allowed = (doc_keys[:, None] == doc_keys[None, :]) & (
        flat_index[:, None] >= flat_index[None, :]
    )
    grouped = grouped.reshape(flat_count, width)
    cotangent = cotangent.reshape(flat_count, width)

    def run_layer(hidden_in, steer_vec):
        return layer_forward(hidden_in, steer_vec, gain_row, full_qkv, full_out, tables, allowed)

    zero_block = jnp.zeros((flat_count, width), jnp.bfloat16)
    zero_proj = jnp.zeros((flat_count, full_qkv.shape[1]), jnp.float32)
    forward_route = [(i, i + 1) for i in range(section_count - 1)]
    backward_route = [(i + 1, i) for i in range(section_count - 1)]

    def forward_step(carry, unused):
        hidden_in, kept, produced, saved, step = carry
        active = section_idx == step
        kept = jnp.where(active, hidden_in, kept)
        hidden_new, projected = lax.cond(
            active, lambda: run_layer(hidden_in, steering), lambda: (zero_block, zero_proj)
        )
        produced = jnp.where(active, hidden_new, produced)
        saved = jnp.where(active, projected, saved)
        sent = lax.ppermute(hidden_new, "section", forward_route)
        return ((sent, kept, produced, saved, step + 1), None)

    (unused_in, kept, produced, saved, unused_step), unused_ys = lax.scan(
        forward_step,
        (grouped, zero_block, zero_block, zero_proj, jnp.int32(0)),
        None,
        length=section_count,
    )

    def backward_step(carry, unused):
        upstream, grad_sum, step = carry
        active = section_idx == step

        def differentiate():
            return layer_backward(
                kept, steering, saved, upstream, gain_row, full_qkv, full_out, tables, allowed
            )

        grad_in, steer_part = lax.cond(
            active, differentiate, lambda: (zero_block, jnp.zeros_like(steering))
        )
        sent = lax.ppermute(grad_in, "section", backward_route)
        return ((sent, grad_sum + steer_part, step - 1), None)

    (unused_grad, grad_sum, unused_step), unused_zs = lax.scan(
        backward_step,
        (cotangent, jnp.zeros_like(steering), jnp.int32(section_count - 1)),
        None,
        length=section_count,
    )

    total = butterfly_sum(grad_sum, "dp")
    return (produced.reshape(1, micro_count, row_count, width), total[None])


def solution(mesh):
    in_specs = (
        P(None, "dp", None),
        P(),
        P(None, "dp"),
        P(None, "dp", None),
        P("section", None),
        P("section", None),
        P("section", "dp", None),
        P("section", "dp", None),
        P("section", None, "dp"),
    )
    out_specs = (P("section", None, "dp", None), P("section", None))
    return jax.shard_map(body, mesh=mesh, in_specs=in_specs, out_specs=out_specs, check_vma=False)
```

```python
import jax
import jax.numpy as jnp
from jax import lax
from jax.sharding import PartitionSpec as P

HD = 64


ROPE_BASE = 500000.0
EPSILON = 1e-05
MASKED = -1e30


def rope_tables(positions):
    half_size = HD // 2
    freq_index = jnp.arange(half_size, dtype=jnp.float32)
    inverse = ROPE_BASE ** (-2.0 * freq_index / HD)
    angles = positions.astype(jnp.float32)[..., None] * inverse
    return (jnp.cos(angles)[..., None, :], jnp.sin(angles)[..., None, :])


def rotate(values, tables):
    half_size = values.shape[-1] // 2
    cosine, sine_part = tables
    first_half = values[..., :half_size]
    second = values[..., half_size:]
    return jnp.concatenate(
        [first_half * cosine - second * sine_part, second * cosine + first_half * sine_part],
        axis=-1,
    )


def normalize(hidden_in, steering, gain_row):
    residual = hidden_in.astype(jnp.float32) + steering
    normed = (
        residual
        * lax.rsqrt(jnp.mean(residual * residual, axis=-1, keepdims=True) + EPSILON)
        * gain_row
    ).astype(jnp.bfloat16)
    return (residual, normed)


def rope_stage(projected_in, tables, query_heads):
    row_count = projected_in.shape[0]
    head_size = HD
    query_cols = query_heads * head_size
    kv_heads = (projected_in.shape[1] - query_cols) // (2 * head_size)
    group_size = query_heads // kv_heads
    queries = projected_in[:, :query_cols].reshape(row_count, query_heads, head_size)
    keyval = projected_in[:, query_cols:]
    key_rows = rotate(
        keyval[:, : kv_heads * head_size].reshape(row_count, kv_heads, head_size), tables
    ).astype(jnp.bfloat16)
    values = (
        keyval[:, kv_heads * head_size :]
        .reshape(row_count, kv_heads, head_size)
        .astype(jnp.bfloat16)
    )
    queries = (
        rotate(queries, tables)
        .astype(jnp.bfloat16)
        .reshape(row_count, kv_heads, group_size, head_size)
    )
    return (queries, key_rows, values)


def attend(queries, key_rows, values, allowed):
    row_count, kv_heads, group_size, head_size = queries.shape
    scores = jnp.einsum(
        "rkgd,skd->kgrs", queries, key_rows, preferred_element_type=jnp.float32
    ) * head_size ** (-0.5)
    scores = jnp.where(allowed[None, None], scores, MASKED)
    peak = jnp.max(scores, axis=-1, keepdims=True)
    weights = jnp.exp(scores - peak)
    weights = (weights / jnp.sum(weights, axis=-1, keepdims=True)).astype(jnp.bfloat16)
    mixed_heads = jnp.einsum(
        "kgrs,skd->rkgd", weights, values, preferred_element_type=jnp.float32
    ).astype(jnp.bfloat16)
    return mixed_heads.reshape(row_count, kv_heads * group_size * head_size)


def project_in(normed, w_qkv):
    return jnp.dot(normed, w_qkv, preferred_element_type=jnp.float32)


def project_out(residual, mixed_heads, w_out):
    return (residual + jnp.dot(mixed_heads, w_out, preferred_element_type=jnp.float32)).astype(
        jnp.bfloat16
    )


def layer_forward(hidden_in, steering, gain_row, w_qkv, w_out, tables, allowed):
    residual, normed = normalize(hidden_in, steering, gain_row)
    projected_in = project_in(normed, w_qkv)
    rotated = rope_stage(projected_in, tables, w_out.shape[0] // HD)
    mixed_heads = attend(*rotated, allowed)
    return (project_out(residual, mixed_heads, w_out), rotated)


def layer_backward(hidden_in, steering, rotated, upstream, gain_row, w_qkv, w_out, tables, allowed):
    query_heads = w_out.shape[0] // HD
    (residual, normed), normalize_pull = jax.vjp(
        lambda h, s: normalize(h, s, gain_row), hidden_in, steering
    )
    mixed_heads, attend_pull = jax.vjp(lambda q, k, v: attend(q, k, v, allowed), *rotated)
    unused_out, out_pull = jax.vjp(
        lambda r, m: project_out(r, m, w_out), residual, mixed_heads
    )
    grad_residual, grad_mixed = out_pull(upstream)
    grad_rotated = attend_pull(grad_mixed)
    linear_point = jnp.zeros((hidden_in.shape[0], w_qkv.shape[1]), jnp.float32)
    unused_rot, rope_pull = jax.vjp(
        lambda p: rope_stage(p, tables, query_heads), linear_point
    )
    (grad_projected,) = rope_pull(grad_rotated)
    unused_proj, in_pull = jax.vjp(lambda n: project_in(n, w_qkv), normed)
    (grad_normed,) = in_pull(grad_projected)
    return normalize_pull((grad_residual, grad_normed))


def butterfly_sum(values, axis):
    count = lax.axis_size(axis)
    distance = 1
    while distance < count:
        route = [(i, i ^ distance) for i in range(count)]
        values = values + lax.ppermute(values, axis, route)
        distance *= 2
    return values


def plan_slots(target, device, row_count, capacity, dp_count):
    target_grid = target.reshape(dp_count, row_count)
    target_dev = target_grid // row_count
    target_off = target_grid % row_count
    row_order = jnp.arange(row_count, dtype=jnp.int32)
    matching = target_dev[:, :, None] == target_dev[:, None, :]
    earlier = row_order[None, :] < row_order[:, None]
    rank_ids = jnp.sum((matching & earlier[None]).astype(jnp.int32), axis=2)
    slot_ids = target_dev * capacity + rank_ids
    own_slot = lax.dynamic_index_in_dim(slot_ids, device, 0, keepdims=False)
    column_ids = jnp.arange(dp_count, dtype=jnp.int32)[:, None] * capacity + rank_ids
    landing = (target_dev == device)[None] & (target_off[None] == row_order[:, None, None])
    source_col = jnp.sum(jnp.where(landing, column_ids[None], 0), axis=(1, 2))
    return (own_slot, source_col)


def pack_rows(source_rows, own_slot, slot_count):
    selector = (jnp.arange(slot_count, dtype=jnp.int32)[:, None] == own_slot[None, :]).astype(
        jnp.bfloat16
    )
    return jnp.dot(selector, source_rows, preferred_element_type=jnp.float32).astype(jnp.bfloat16)


def unpack_rows(arrived, source_col):
    selector = (
        source_col[:, None] == jnp.arange(arrived.shape[0], dtype=jnp.int32)[None, :]
    ).astype(jnp.bfloat16)
    return jnp.dot(selector, arrived, preferred_element_type=jnp.float32).astype(jnp.bfloat16)


def body(resid_in, dest_row, doc_ids, cotangent, gain, steer, w_query, w_keyval, w_out):
    dp_count = lax.axis_size("dp")
    section_count = lax.axis_size("section")
    device = lax.axis_index("dp")
    section_idx = lax.axis_index("section")
    micro_count, row_count, width = resid_in.shape
    capacity = row_count // dp_count + 1
    slot_count = dp_count * capacity
    full_qkv = lax.all_gather(
        jnp.concatenate([w_query[0], w_keyval[0]], axis=1), "dp", axis=0, tiled=True
    )
    full_out = lax.all_gather(w_out[0], "dp", axis=1, tiled=True)
    gain_row = gain[0]
    steering = steer[0]
    plans = [
        plan_slots(dest_row[micro_idx], device, row_count, capacity, dp_count)
        for micro_idx in range(micro_count)
    ]
    packed = jnp.stack(
        [
            pack_rows(resid_in[micro_idx], plans[micro_idx][0], slot_count).reshape(
                dp_count, capacity, width
            )
            for micro_idx in range(micro_count)
        ],
        axis=1,
    )
    arrived = lax.all_to_all(packed, "dp", split_axis=0, concat_axis=0, tiled=True)
    grouped = jnp.stack(
        [
            unpack_rows(arrived[:, micro_idx].reshape(slot_count, width), plans[micro_idx][1])
            for micro_idx in range(micro_count)
        ]
    )
    global_rows = device * row_count + jnp.arange(row_count, dtype=jnp.int32)
    flat_count = micro_count * row_count
    tables = rope_tables((global_rows[None, :] - doc_ids).reshape(flat_count))
    micro_of = jnp.arange(flat_count, dtype=jnp.int32) // row_count
    doc_keys = doc_ids.reshape(flat_count) + micro_of * (dp_count * row_count)
    flat_index = jnp.arange(flat_count, dtype=jnp.int32)
    allowed = (doc_keys[:, None] == doc_keys[None, :]) & (
        flat_index[:, None] >= flat_index[None, :]
    )
    grouped = grouped.reshape(flat_count, width)
    cotangent = cotangent.reshape(flat_count, width)

    def run_layer(hidden_in, steer_vec):
        return layer_forward(hidden_in, steer_vec, gain_row, full_qkv, full_out, tables, allowed)

    zero_block = jnp.zeros((flat_count, width), jnp.bfloat16)
    zero_proj = jax.tree_util.tree_map(
        lambda leaf: jnp.zeros(leaf.shape, leaf.dtype),
        jax.eval_shape(lambda: run_layer(zero_block, steering)[1]),
    )
    forward_route = [(i, i + 1) for i in range(section_count - 1)]
    backward_route = [(i + 1, i) for i in range(section_count - 1)]

    def forward_step(carry, unused):
        hidden_in, kept, produced, saved, step = carry
        active = section_idx == step
        kept = jnp.where(active, hidden_in, kept)
        hidden_new, projected = lax.cond(
            active, lambda: run_layer(hidden_in, steering), lambda: (zero_block, zero_proj)
        )
        produced = jnp.where(active, hidden_new, produced)
        saved = jax.tree_util.tree_map(
            lambda new, old: jnp.where(active, new, old), projected, saved
        )
        sent = lax.ppermute(hidden_new, "section", forward_route)
        return ((sent, kept, produced, saved, step + 1), None)

    (unused_in, kept, produced, saved, unused_step), unused_ys = lax.scan(
        forward_step,
        (grouped, zero_block, zero_block, zero_proj, jnp.int32(0)),
        None,
        length=section_count,
    )

    def backward_step(carry, unused):
        upstream, grad_sum, step = carry
        active = section_idx == step

        def differentiate():
            return layer_backward(
                kept, steering, saved, upstream, gain_row, full_qkv, full_out, tables, allowed
            )

        grad_in, steer_part = lax.cond(
            active, differentiate, lambda: (zero_block, jnp.zeros_like(steering))
        )
        sent = lax.ppermute(grad_in, "section", backward_route)
        return ((sent, grad_sum + steer_part, step - 1), None)

    (unused_grad, grad_sum, unused_step), unused_zs = lax.scan(
        backward_step,
        (cotangent, jnp.zeros_like(steering), jnp.int32(section_count - 1)),
        None,
        length=section_count,
    )

    total = butterfly_sum(grad_sum, "dp")
    return (produced.reshape(1, micro_count, row_count, width), total[None])


def solution(mesh):
    in_specs = (
        P(None, "dp", None),
        P(),
        P(None, "dp"),
        P(None, "dp", None),
        P("section", None),
        P("section", None),
        P("section", "dp", None),
        P("section", "dp", None),
        P("section", None, "dp"),
    )
    out_specs = (P("section", None, "dp", None), P("section", None))
    return jax.shard_map(body, mesh=mesh, in_specs=in_specs, out_specs=out_specs, check_vma=False)
```

```python
import jax
import jax.numpy as jnp
from jax import lax
from jax.sharding import PartitionSpec as P

HD = 64


ROPE_BASE = 500000.0
EPSILON = 1e-05
MASKED = -1e30


def rope_tables(positions):
    half_size = HD // 2
    freq_index = jnp.arange(half_size, dtype=jnp.float32)
    inverse = ROPE_BASE ** (-2.0 * freq_index / HD)
    angles = positions.astype(jnp.float32)[..., None] * inverse
    return (jnp.cos(angles)[..., None, :], jnp.sin(angles)[..., None, :])


def rotate(values, tables):
    half_size = values.shape[-1] // 2
    cosine, sine_part = tables
    first_half = values[..., :half_size]
    second = values[..., half_size:]
    return jnp.concatenate(
        [first_half * cosine - second * sine_part, second * cosine + first_half * sine_part],
        axis=-1,
    )


def normalize(hidden_in, steering, gain_row):
    residual = hidden_in.astype(jnp.float32) + steering
    normed = (
        residual
        * lax.rsqrt(jnp.mean(residual * residual, axis=-1, keepdims=True) + EPSILON)
        * gain_row
    ).astype(jnp.bfloat16)
    return (residual, normed)


def attend(projected_in, tables, allowed, query_heads):
    row_count = projected_in.shape[0]
    head_size = HD
    query_cols = query_heads * head_size
    kv_heads = (projected_in.shape[1] - query_cols) // (2 * head_size)
    group_size = query_heads // kv_heads
    queries = projected_in[:, :query_cols].reshape(row_count, query_heads, head_size)
    keyval = projected_in[:, query_cols:]
    key_rows = rotate(
        keyval[:, : kv_heads * head_size].reshape(row_count, kv_heads, head_size), tables
    ).astype(jnp.bfloat16)
    values = (
        keyval[:, kv_heads * head_size :]
        .reshape(row_count, kv_heads, head_size)
        .astype(jnp.bfloat16)
    )
    queries = (
        rotate(queries, tables)
        .astype(jnp.bfloat16)
        .reshape(row_count, kv_heads, group_size, head_size)
    )
    scores = jnp.einsum(
        "rkgd,skd->kgrs", queries, key_rows, preferred_element_type=jnp.float32
    ) * head_size ** (-0.5)
    scores = jnp.where(allowed[None, None], scores, MASKED)
    peak = jnp.max(scores, axis=-1, keepdims=True)
    weights = jnp.exp(scores - peak)
    weights = (weights / jnp.sum(weights, axis=-1, keepdims=True)).astype(jnp.bfloat16)
    mixed_heads = jnp.einsum(
        "kgrs,skd->rkgd", weights, values, preferred_element_type=jnp.float32
    ).astype(jnp.bfloat16)
    return mixed_heads.reshape(row_count, query_heads * head_size)


def project_in(normed, w_qkv):
    return jnp.dot(normed, w_qkv, preferred_element_type=jnp.float32)


def project_out(residual, mixed_heads, w_out):
    return (residual + jnp.dot(mixed_heads, w_out, preferred_element_type=jnp.float32)).astype(
        jnp.bfloat16
    )


def layer_forward(hidden_in, steering, gain_row, w_qkv, w_out, tables, allowed):
    residual, normed = normalize(hidden_in, steering, gain_row)
    projected_in = project_in(normed, w_qkv)
    mixed_heads = attend(projected_in, tables, allowed, w_out.shape[0] // HD)
    return (project_out(residual, mixed_heads, w_out), projected_in)


def layer_backward(
    hidden_in, steering, projected_in, upstream, gain_row, w_qkv, w_out, tables, allowed
):
    query_heads = w_out.shape[0] // HD
    (residual, normed), normalize_pull = jax.vjp(
        lambda h, s: normalize(h, s, gain_row), hidden_in, steering
    )
    mixed_heads, attend_pull = jax.vjp(
        lambda p: attend(p, tables, allowed, query_heads), projected_in
    )
    unused_out, out_pull = jax.vjp(
        lambda r, m: project_out(r, m, w_out), residual, mixed_heads
    )
    grad_residual, grad_mixed = out_pull(upstream)
    (grad_projected,) = attend_pull(grad_mixed)
    unused_proj, in_pull = jax.vjp(lambda n: project_in(n, w_qkv), normed)
    (grad_normed,) = in_pull(grad_projected)
    return normalize_pull((grad_residual, grad_normed))


def butterfly_sum(values, axis):
    count = lax.axis_size(axis)
    distance = 1
    while distance < count:
        route = [(i, i ^ distance) for i in range(count)]
        values = values + lax.ppermute(values, axis, route)
        distance *= 2
    return values


def plan_slots(target, device, row_count, capacity, dp_count):
    target_grid = target.reshape(dp_count, row_count)
    target_dev = target_grid // row_count
    target_off = target_grid % row_count
    row_order = jnp.arange(row_count, dtype=jnp.int32)
    matching = target_dev[:, :, None] == target_dev[:, None, :]
    earlier = row_order[None, :] < row_order[:, None]
    rank_ids = jnp.sum((matching & earlier[None]).astype(jnp.int32), axis=2)
    slot_ids = target_dev * capacity + rank_ids
    own_slot = lax.dynamic_index_in_dim(slot_ids, device, 0, keepdims=False)
    column_ids = jnp.arange(dp_count, dtype=jnp.int32)[:, None] * capacity + rank_ids
    landing = (target_dev == device)[None] & (target_off[None] == row_order[:, None, None])
    source_col = jnp.sum(jnp.where(landing, column_ids[None], 0), axis=(1, 2))
    return (own_slot, source_col)


def pack_rows(source_rows, own_slot, slot_count):
    selector = (jnp.arange(slot_count, dtype=jnp.int32)[:, None] == own_slot[None, :]).astype(
        jnp.bfloat16
    )
    return jnp.dot(selector, source_rows, preferred_element_type=jnp.float32).astype(jnp.bfloat16)


def unpack_rows(arrived, source_col):
    selector = (
        source_col[:, None] == jnp.arange(arrived.shape[0], dtype=jnp.int32)[None, :]
    ).astype(jnp.bfloat16)
    return jnp.dot(selector, arrived, preferred_element_type=jnp.float32).astype(jnp.bfloat16)


def body(resid_in, dest_row, doc_ids, cotangent, gain, steer, w_query, w_keyval, w_out):
    dp_count = lax.axis_size("dp")
    section_count = lax.axis_size("section")
    device = lax.axis_index("dp")
    section_idx = lax.axis_index("section")
    micro_count, row_count, width = resid_in.shape
    capacity = row_count // dp_count + 1
    slot_count = dp_count * capacity
    full_qkv = lax.all_gather(
        jnp.concatenate([w_query[0], w_keyval[0]], axis=1), "dp", axis=0, tiled=True
    )
    full_out = lax.all_gather(w_out[0], "dp", axis=1, tiled=True)
    gain_row = gain[0]
    steering = steer[0]
    plans = [
        plan_slots(dest_row[micro_idx], device, row_count, capacity, dp_count)
        for micro_idx in range(micro_count)
    ]
    packed = jnp.stack(
        [
            pack_rows(resid_in[micro_idx], plans[micro_idx][0], slot_count).reshape(
                dp_count, capacity, width
            )
            for micro_idx in range(micro_count)
        ],
        axis=1,
    )
    arrived = lax.all_to_all(packed, "dp", split_axis=0, concat_axis=0, tiled=True)
    grouped = jnp.stack(
        [
            unpack_rows(arrived[:, micro_idx].reshape(slot_count, width), plans[micro_idx][1])
            for micro_idx in range(micro_count)
        ]
    )
    global_rows = device * row_count + jnp.arange(row_count, dtype=jnp.int32)
    flat_count = micro_count * row_count
    tables = rope_tables((global_rows[None, :] - doc_ids).reshape(flat_count))
    micro_of = jnp.arange(flat_count, dtype=jnp.int32) // row_count
    doc_keys = doc_ids.reshape(flat_count) + micro_of * (dp_count * row_count)
    flat_index = jnp.arange(flat_count, dtype=jnp.int32)
    allowed = (doc_keys[:, None] == doc_keys[None, :]) & (
        flat_index[:, None] >= flat_index[None, :]
    )
    grouped = grouped.reshape(flat_count, width)
    cotangent = cotangent.reshape(flat_count, width)

    def run_layer(hidden_in, steer_vec):
        return layer_forward(hidden_in, steer_vec, gain_row, full_qkv, full_out, tables, allowed)

    zero_block = jnp.zeros((flat_count, width), jnp.bfloat16)
    zero_proj = jnp.zeros((flat_count, full_qkv.shape[1]), jnp.float32)

    def precompute(hidden_in):
        return project_in(normalize(hidden_in, steering, gain_row)[1], full_qkv)
    forward_route = [(i, i + 1) for i in range(section_count - 1)]
    backward_route = [(i + 1, i) for i in range(section_count - 1)]

    def forward_step(carry, unused):
        hidden_in, kept, produced, step = carry
        active = section_idx == step
        kept = jnp.where(active, hidden_in, kept)
        hidden_new = lax.cond(active, lambda: run_layer(hidden_in, steering)[0], lambda: zero_block)
        produced = jnp.where(active, hidden_new, produced)
        sent = lax.ppermute(hidden_new, "section", forward_route)
        return ((sent, kept, produced, step + 1), None)

    (unused_in, kept, produced, unused_step), unused_ys = lax.scan(
        forward_step, (grouped, zero_block, zero_block, jnp.int32(0)), None, length=section_count
    )
    first_saved = lax.cond(
        section_idx == section_count - 1, lambda: precompute(kept), lambda: zero_proj
    )

    def backward_step(carry, unused):
        upstream, grad_sum, step, saved = carry
        active = section_idx == step

        def differentiate():
            return layer_backward(
                kept, steering, saved, upstream, gain_row, full_qkv, full_out, tables, allowed
            )

        grad_in, steer_part = lax.cond(
            active, differentiate, lambda: (zero_block, jnp.zeros_like(steering))
        )
        sent = lax.ppermute(grad_in, "section", backward_route)
        next_saved = lax.cond(
            section_idx == step - 1, lambda: precompute(kept), lambda: zero_proj
        )
        return ((sent, grad_sum + steer_part, step - 1, next_saved), None)

    (unused_grad, grad_sum, unused_step, unused_saved), unused_zs = lax.scan(
        backward_step,
        (cotangent, jnp.zeros_like(steering), jnp.int32(section_count - 1), first_saved),
        None,
        length=section_count,
    )

    total = butterfly_sum(grad_sum, "dp")
    return (produced.reshape(1, micro_count, row_count, width), total[None])


def solution(mesh):
    in_specs = (
        P(None, "dp", None),
        P(),
        P(None, "dp"),
        P(None, "dp", None),
        P("section", None),
        P("section", None),
        P("section", "dp", None),
        P("section", "dp", None),
        P("section", None, "dp"),
    )
    out_specs = (P("section", None, "dp", None), P("section", None))
    return jax.shard_map(body, mesh=mesh, in_specs=in_specs, out_specs=out_specs, check_vma=False)
```

```python
import jax
import jax.numpy as jnp
from jax import lax
from jax.sharding import PartitionSpec as P

HD = 64


ROPE_BASE = 500000.0
EPSILON = 1e-05
MASKED = -1e30


def rope_tables(positions):
    half_size = HD // 2
    freq_index = jnp.arange(half_size, dtype=jnp.float32)
    inverse = ROPE_BASE ** (-2.0 * freq_index / HD)
    angles = positions.astype(jnp.float32)[..., None] * inverse
    return (jnp.cos(angles)[..., None, :], jnp.sin(angles)[..., None, :])


def rotate(values, tables):
    half_size = values.shape[-1] // 2
    cosine, sine_part = tables
    first_half = values[..., :half_size]
    second = values[..., half_size:]
    return jnp.concatenate(
        [first_half * cosine - second * sine_part, second * cosine + first_half * sine_part],
        axis=-1,
    )


def normalize(hidden_in, steering, gain_row):
    residual = hidden_in.astype(jnp.float32) + steering
    normed = (
        residual
        * lax.rsqrt(jnp.mean(residual * residual, axis=-1, keepdims=True) + EPSILON)
        * gain_row
    ).astype(jnp.bfloat16)
    return (residual, normed)


def attend(projected_in, tables, allowed, query_heads):
    row_count = projected_in.shape[0]
    head_size = HD
    query_cols = query_heads * head_size
    kv_heads = (projected_in.shape[1] - query_cols) // (2 * head_size)
    group_size = query_heads // kv_heads
    queries = projected_in[:, :query_cols].reshape(row_count, query_heads, head_size)
    keyval = projected_in[:, query_cols:]
    key_rows = rotate(
        keyval[:, : kv_heads * head_size].reshape(row_count, kv_heads, head_size), tables
    ).astype(jnp.bfloat16)
    values = (
        keyval[:, kv_heads * head_size :]
        .reshape(row_count, kv_heads, head_size)
        .astype(jnp.bfloat16)
    )
    queries = (
        rotate(queries, tables)
        .astype(jnp.bfloat16)
        .reshape(row_count, kv_heads, group_size, head_size)
    )
    scores = jnp.einsum(
        "rkgd,skd->kgrs", queries, key_rows, preferred_element_type=jnp.float32
    ) * head_size ** (-0.5)
    scores = jnp.where(allowed[None, None], scores, MASKED)
    peak = jnp.max(scores, axis=-1, keepdims=True)
    weights = jnp.exp(scores - peak)
    weights = (weights / jnp.sum(weights, axis=-1, keepdims=True)).astype(jnp.bfloat16)
    mixed_heads = jnp.einsum(
        "kgrs,skd->rkgd", weights, values, preferred_element_type=jnp.float32
    ).astype(jnp.bfloat16)
    return mixed_heads.reshape(row_count, query_heads * head_size)


def project_in(normed, w_qkv):
    return jnp.dot(normed, w_qkv, preferred_element_type=jnp.float32)


def project_out(residual, mixed_heads, w_out):
    return (residual + jnp.dot(mixed_heads, w_out, preferred_element_type=jnp.float32)).astype(
        jnp.bfloat16
    )


def layer_forward(hidden_in, steering, gain_row, w_qkv, w_out, tables, allowed):
    residual, normed = normalize(hidden_in, steering, gain_row)
    projected_in = project_in(normed, w_qkv)
    mixed_heads = attend(projected_in, tables, allowed, w_out.shape[0] // HD)
    return (project_out(residual, mixed_heads, w_out), projected_in)


def layer_backward(
    hidden_in, steering, projected_in, upstream, gain_row, w_qkv, w_out, tables, allowed
):
    query_heads = w_out.shape[0] // HD
    (residual, normed), normalize_pull = jax.vjp(
        lambda h, s: normalize(h, s, gain_row), hidden_in, steering
    )
    mixed_heads, attend_pull = jax.vjp(
        lambda p: attend(p, tables, allowed, query_heads), projected_in
    )
    unused_out, out_pull = jax.vjp(
        lambda r, m: project_out(r, m, w_out), residual, mixed_heads
    )
    grad_residual, grad_mixed = out_pull(upstream)
    (grad_projected,) = attend_pull(grad_mixed)
    unused_proj, in_pull = jax.vjp(lambda n: project_in(n, w_qkv), normed)
    (grad_normed,) = in_pull(grad_projected)
    return normalize_pull((grad_residual, grad_normed))


def butterfly_sum(values, axis):
    count = lax.axis_size(axis)
    distance = 1
    while distance < count:
        route = [(i, i ^ distance) for i in range(count)]
        values = values + lax.ppermute(values, axis, route)
        distance *= 2
    return values


def plan_slots(target, device, row_count, capacity, dp_count):
    target_grid = target.reshape(dp_count, row_count)
    target_dev = target_grid // row_count
    target_off = target_grid % row_count
    row_order = jnp.arange(row_count, dtype=jnp.int32)
    matching = target_dev[:, :, None] == target_dev[:, None, :]
    earlier = row_order[None, :] < row_order[:, None]
    rank_ids = jnp.sum((matching & earlier[None]).astype(jnp.int32), axis=2)
    slot_ids = target_dev * capacity + rank_ids
    own_slot = lax.dynamic_index_in_dim(slot_ids, device, 0, keepdims=False)
    column_ids = jnp.arange(dp_count, dtype=jnp.int32)[:, None] * capacity + rank_ids
    landing = (target_dev == device)[None] & (target_off[None] == row_order[:, None, None])
    source_col = jnp.sum(jnp.where(landing, column_ids[None], 0), axis=(1, 2))
    return (own_slot, source_col)


def pack_rows(source_rows, own_slot, slot_count):
    selector = (jnp.arange(slot_count, dtype=jnp.int32)[:, None] == own_slot[None, :]).astype(
        jnp.bfloat16
    )
    return jnp.dot(selector, source_rows, preferred_element_type=jnp.float32).astype(jnp.bfloat16)


def unpack_rows(arrived, source_col):
    selector = (
        source_col[:, None] == jnp.arange(arrived.shape[0], dtype=jnp.int32)[None, :]
    ).astype(jnp.bfloat16)
    return jnp.dot(selector, arrived, preferred_element_type=jnp.float32).astype(jnp.bfloat16)


def body(resid_in, dest_row, doc_ids, cotangent, gain, steer, w_query, w_keyval, w_out):
    dp_count = lax.axis_size("dp")
    section_count = lax.axis_size("section")
    device = lax.axis_index("dp")
    section_idx = lax.axis_index("section")
    micro_count, row_count, width = resid_in.shape
    capacity = row_count // dp_count + 1
    slot_count = dp_count * capacity
    full_qkv = lax.all_gather(
        jnp.concatenate([w_query[0], w_keyval[0]], axis=1), "dp", axis=0, tiled=True
    )
    out_block = w_out[0]
    spread = jnp.broadcast_to(out_block[None], (dp_count,) + out_block.shape)
    arrived_out = lax.all_to_all(spread, "dp", split_axis=0, concat_axis=0, tiled=True)
    full_out = lax.optimization_barrier(
        arrived_out.transpose(1, 0, 2).reshape(out_block.shape[0], dp_count * out_block.shape[1])
    )
    gain_row = gain[0]
    steering = steer[0]
    plans = [
        plan_slots(dest_row[micro_idx], device, row_count, capacity, dp_count)
        for micro_idx in range(micro_count)
    ]
    packed = jnp.stack(
        [
            pack_rows(resid_in[micro_idx], plans[micro_idx][0], slot_count).reshape(
                dp_count, capacity, width
            )
            for micro_idx in range(micro_count)
        ],
        axis=1,
    )
    arrived = lax.all_to_all(packed, "dp", split_axis=0, concat_axis=0, tiled=True)
    grouped = jnp.stack(
        [
            unpack_rows(arrived[:, micro_idx].reshape(slot_count, width), plans[micro_idx][1])
            for micro_idx in range(micro_count)
        ]
    )
    global_rows = device * row_count + jnp.arange(row_count, dtype=jnp.int32)
    flat_count = micro_count * row_count
    tables = rope_tables((global_rows[None, :] - doc_ids).reshape(flat_count))
    micro_of = jnp.arange(flat_count, dtype=jnp.int32) // row_count
    doc_keys = doc_ids.reshape(flat_count) + micro_of * (dp_count * row_count)
    flat_index = jnp.arange(flat_count, dtype=jnp.int32)
    allowed = (doc_keys[:, None] == doc_keys[None, :]) & (
        flat_index[:, None] >= flat_index[None, :]
    )
    grouped = grouped.reshape(flat_count, width)
    cotangent = cotangent.reshape(flat_count, width)

    def run_layer(hidden_in, steer_vec):
        return layer_forward(hidden_in, steer_vec, gain_row, full_qkv, full_out, tables, allowed)

    zero_block = jnp.zeros((flat_count, width), jnp.bfloat16)
    zero_proj = jnp.zeros((flat_count, full_qkv.shape[1]), jnp.float32)

    def precompute(hidden_in):
        return project_in(normalize(hidden_in, steering, gain_row)[1], full_qkv)
    forward_route = [(i, i + 1) for i in range(section_count - 1)]
    backward_route = [(i + 1, i) for i in range(section_count - 1)]

    def forward_step(carry, unused):
        hidden_in, kept, produced, step = carry
        active = section_idx == step
        kept = jnp.where(active, hidden_in, kept)
        hidden_new = lax.cond(active, lambda: run_layer(hidden_in, steering)[0], lambda: zero_block)
        produced = jnp.where(active, hidden_new, produced)
        sent = lax.ppermute(hidden_new, "section", forward_route)
        return ((sent, kept, produced, step + 1), None)

    (unused_in, kept, produced, unused_step), unused_ys = lax.scan(
        forward_step, (grouped, zero_block, zero_block, jnp.int32(0)), None, length=section_count
    )
    first_saved = lax.cond(
        section_idx == section_count - 1, lambda: precompute(kept), lambda: zero_proj
    )

    def backward_step(carry, unused):
        upstream, grad_sum, step, saved = carry
        active = section_idx == step

        def differentiate():
            return layer_backward(
                kept, steering, saved, upstream, gain_row, full_qkv, full_out, tables, allowed
            )

        grad_in, steer_part = lax.cond(
            active, differentiate, lambda: (zero_block, jnp.zeros_like(steering))
        )
        sent = lax.ppermute(grad_in, "section", backward_route)
        next_saved = lax.cond(
            section_idx == step - 1, lambda: precompute(kept), lambda: zero_proj
        )
        return ((sent, grad_sum + steer_part, step - 1, next_saved), None)

    (unused_grad, grad_sum, unused_step, unused_saved), unused_zs = lax.scan(
        backward_step,
        (cotangent, jnp.zeros_like(steering), jnp.int32(section_count - 1), first_saved),
        None,
        length=section_count,
    )

    total = butterfly_sum(grad_sum, "dp")
    return (produced.reshape(1, micro_count, row_count, width), total[None])


def solution(mesh):
    in_specs = (
        P(None, "dp", None),
        P(),
        P(None, "dp"),
        P(None, "dp", None),
        P("section", None),
        P("section", None),
        P("section", "dp", None),
        P("section", "dp", None),
        P("section", None, "dp"),
    )
    out_specs = (P("section", None, "dp", None), P("section", None))
    return jax.shard_map(body, mesh=mesh, in_specs=in_specs, out_specs=out_specs, check_vma=False)
```

```python
import jax
import jax.numpy as jnp
from jax import lax
from jax.sharding import PartitionSpec as P

HD = 64


ROPE_BASE = 500000.0
EPSILON = 1e-05
MASKED = -1e30


def rope_tables(positions):
    half_size = HD // 2
    freq_index = jnp.arange(half_size, dtype=jnp.float32)
    inverse = ROPE_BASE ** (-2.0 * freq_index / HD)
    angles = positions.astype(jnp.float32)[..., None] * inverse
    return (jnp.cos(angles)[..., None, :], jnp.sin(angles)[..., None, :])


def rotate(values, tables):
    half_size = values.shape[-1] // 2
    cosine, sine_part = tables
    first_half = values[..., :half_size]
    second = values[..., half_size:]
    return jnp.concatenate(
        [first_half * cosine - second * sine_part, second * cosine + first_half * sine_part],
        axis=-1,
    )


def normalize(hidden_in, steering, gain_row):
    residual = hidden_in.astype(jnp.float32) + steering
    normed = (
        residual
        * lax.rsqrt(jnp.mean(residual * residual, axis=-1, keepdims=True) + EPSILON)
        * gain_row
    ).astype(jnp.bfloat16)
    return (residual, normed)


def attend(projected_in, tables, allowed, query_heads):
    row_count = projected_in.shape[0]
    head_size = HD
    query_cols = query_heads * head_size
    kv_heads = (projected_in.shape[1] - query_cols) // (2 * head_size)
    group_size = query_heads // kv_heads
    queries = projected_in[:, :query_cols].reshape(row_count, query_heads, head_size)
    keyval = projected_in[:, query_cols:]
    key_rows = rotate(
        keyval[:, : kv_heads * head_size].reshape(row_count, kv_heads, head_size), tables
    ).astype(jnp.bfloat16)
    values = (
        keyval[:, kv_heads * head_size :]
        .reshape(row_count, kv_heads, head_size)
        .astype(jnp.bfloat16)
    )
    queries = (
        rotate(queries, tables)
        .astype(jnp.bfloat16)
        .reshape(row_count, kv_heads, group_size, head_size)
    )
    scores = jnp.einsum(
        "rkgd,skd->kgrs", queries, key_rows, preferred_element_type=jnp.float32
    ) * head_size ** (-0.5)
    scores = jnp.where(allowed[None, None], scores, MASKED)
    peak = jnp.max(scores, axis=-1, keepdims=True)
    weights = jnp.exp(scores - peak)
    weights = (weights / jnp.sum(weights, axis=-1, keepdims=True)).astype(jnp.bfloat16)
    mixed_heads = jnp.einsum(
        "kgrs,skd->rkgd", weights, values, preferred_element_type=jnp.float32
    ).astype(jnp.bfloat16)
    return mixed_heads.reshape(row_count, query_heads * head_size)


def project_in(normed, w_qkv):
    return jnp.dot(normed, w_qkv, preferred_element_type=jnp.float32)


def project_out(residual, mixed_heads, w_out):
    return (residual + jnp.dot(mixed_heads, w_out, preferred_element_type=jnp.float32)).astype(
        jnp.bfloat16
    )


def layer_forward(hidden_in, steering, gain_row, w_qkv, w_out, tables, allowed):
    residual, normed = normalize(hidden_in, steering, gain_row)
    projected_in = project_in(normed, w_qkv)
    mixed_heads = attend(projected_in, tables, allowed, w_out.shape[0] // HD)
    return (project_out(residual, mixed_heads, w_out), projected_in)


def layer_backward(
    hidden_in, steering, projected_in, upstream, gain_row, w_qkv, w_out, tables, allowed
):
    query_heads = w_out.shape[0] // HD
    (residual, normed), normalize_pull = jax.vjp(
        lambda h, s: normalize(h, s, gain_row), hidden_in, steering
    )
    mixed_heads, attend_pull = jax.vjp(
        lambda p: attend(p, tables, allowed, query_heads), projected_in
    )
    unused_out, out_pull = jax.vjp(
        lambda r, m: project_out(r, m, w_out), residual, mixed_heads
    )
    grad_residual, grad_mixed = out_pull(upstream)
    (grad_projected,) = attend_pull(grad_mixed)
    unused_proj, in_pull = jax.vjp(lambda n: project_in(n, w_qkv), normed)
    (grad_normed,) = in_pull(grad_projected)
    return normalize_pull((grad_residual, grad_normed))


def butterfly_sum(values, axis):
    count = lax.axis_size(axis)
    distance = 1
    while distance < count:
        route = [(i, i ^ distance) for i in range(count)]
        values = values + lax.ppermute(values, axis, route)
        distance *= 2
    return values


def plan_slots(target, device, row_count, capacity, dp_count):
    target_grid = target.reshape(dp_count, row_count)
    target_dev = target_grid // row_count
    target_off = target_grid % row_count
    row_order = jnp.arange(row_count, dtype=jnp.int32)
    matching = target_dev[:, :, None] == target_dev[:, None, :]
    earlier = row_order[None, :] < row_order[:, None]
    rank_ids = jnp.sum((matching & earlier[None]).astype(jnp.int32), axis=2)
    slot_ids = target_dev * capacity + rank_ids
    own_slot = lax.dynamic_index_in_dim(slot_ids, device, 0, keepdims=False)
    column_ids = jnp.arange(dp_count, dtype=jnp.int32)[:, None] * capacity + rank_ids
    landing = (target_dev == device)[None] & (target_off[None] == row_order[:, None, None])
    source_col = jnp.sum(jnp.where(landing, column_ids[None], 0), axis=(1, 2))
    return (own_slot, source_col)


def pack_rows(source_rows, own_slot, slot_count):
    selector = (jnp.arange(slot_count, dtype=jnp.int32)[:, None] == own_slot[None, :]).astype(
        jnp.bfloat16
    )
    return jnp.dot(selector, source_rows, preferred_element_type=jnp.float32).astype(jnp.bfloat16)


def unpack_rows(arrived, source_col):
    selector = (
        source_col[:, None] == jnp.arange(arrived.shape[0], dtype=jnp.int32)[None, :]
    ).astype(jnp.bfloat16)
    return jnp.dot(selector, arrived, preferred_element_type=jnp.float32).astype(jnp.bfloat16)


def body(resid_in, dest_row, doc_ids, cotangent, gain, steer, w_query, w_keyval, w_out):
    dp_count = lax.axis_size("dp")
    section_count = lax.axis_size("section")
    device = lax.axis_index("dp")
    section_idx = lax.axis_index("section")
    micro_count, row_count, width = resid_in.shape
    capacity = row_count // dp_count + 1
    slot_count = dp_count * capacity
    full_qkv = lax.all_gather(
        jnp.concatenate([w_query[0], w_keyval[0]], axis=1), "dp", axis=0, tiled=True
    )
    full_out = lax.all_gather(w_out[0], "dp", axis=1, tiled=True)
    gain_row = gain[0]
    steering = steer[0]
    plans = [
        plan_slots(dest_row[micro_idx], device, row_count, capacity, dp_count)
        for micro_idx in range(micro_count)
    ]
    packed = jnp.stack(
        [
            pack_rows(resid_in[micro_idx], plans[micro_idx][0], slot_count).reshape(
                dp_count, capacity, width
            )
            for micro_idx in range(micro_count)
        ],
        axis=1,
    )
    arrived = lax.all_to_all(packed, "dp", split_axis=0, concat_axis=0, tiled=True)
    grouped = jnp.stack(
        [
            unpack_rows(arrived[:, micro_idx].reshape(slot_count, width), plans[micro_idx][1])
            for micro_idx in range(micro_count)
        ]
    )
    global_rows = device * row_count + jnp.arange(row_count, dtype=jnp.int32)
    flat_count = micro_count * row_count
    tables = rope_tables((global_rows[None, :] - doc_ids).reshape(flat_count))
    micro_of = jnp.arange(flat_count, dtype=jnp.int32) // row_count
    doc_keys = doc_ids.reshape(flat_count) + micro_of * (dp_count * row_count)
    flat_index = jnp.arange(flat_count, dtype=jnp.int32)
    allowed = (doc_keys[:, None] == doc_keys[None, :]) & (
        flat_index[:, None] >= flat_index[None, :]
    )
    grouped = grouped.reshape(flat_count, width)
    cotangent = cotangent.reshape(flat_count, width)

    def run_layer(hidden_in, steer_vec):
        return layer_forward(hidden_in, steer_vec, gain_row, full_qkv, full_out, tables, allowed)

    zero_block = jnp.zeros((flat_count, width), jnp.bfloat16)
    zero_proj = jnp.zeros((flat_count, full_qkv.shape[1]), jnp.float32)

    def precompute(hidden_in):
        return project_in(normalize(hidden_in, steering, gain_row)[1], full_qkv)
    forward_route = [(i, i + 1) for i in range(section_count - 1)]
    backward_route = [(i + 1, i) for i in range(section_count - 1)]

    def forward_step(carry, unused):
        hidden_in, step = carry
        active = section_idx == step
        hidden_new = lax.cond(active, lambda: run_layer(hidden_in, steering)[0], lambda: zero_block)
        sent = lax.ppermute(hidden_new, "section", forward_route)
        return ((sent, step + 1), (hidden_in, hidden_new))

    unused_carry, (inputs_seen, outputs_made) = lax.scan(
        forward_step, (grouped, jnp.int32(0)), None, length=section_count
    )
    kept = lax.dynamic_index_in_dim(inputs_seen, section_idx, 0, keepdims=False)
    produced = lax.dynamic_index_in_dim(outputs_made, section_idx, 0, keepdims=False)
    first_saved = lax.cond(
        section_idx == section_count - 1, lambda: precompute(kept), lambda: zero_proj
    )

    def backward_step(carry, unused):
        upstream, grad_sum, step, saved = carry
        active = section_idx == step

        def differentiate():
            return layer_backward(
                kept, steering, saved, upstream, gain_row, full_qkv, full_out, tables, allowed
            )

        grad_in, steer_part = lax.cond(
            active, differentiate, lambda: (zero_block, jnp.zeros_like(steering))
        )
        sent = lax.ppermute(grad_in, "section", backward_route)
        next_saved = lax.cond(
            section_idx == step - 1, lambda: precompute(kept), lambda: zero_proj
        )
        return ((sent, grad_sum + steer_part, step - 1, next_saved), None)

    (unused_grad, grad_sum, unused_step, unused_saved), unused_zs = lax.scan(
        backward_step,
        (cotangent, jnp.zeros_like(steering), jnp.int32(section_count - 1), first_saved),
        None,
        length=section_count,
    )

    total = butterfly_sum(grad_sum, "dp")
    return (produced.reshape(1, micro_count, row_count, width), total[None])


def solution(mesh):
    in_specs = (
        P(None, "dp", None),
        P(),
        P(None, "dp"),
        P(None, "dp", None),
        P("section", None),
        P("section", None),
        P("section", "dp", None),
        P("section", "dp", None),
        P("section", None, "dp"),
    )
    out_specs = (P("section", None, "dp", None), P("section", None))
    return jax.shard_map(body, mesh=mesh, in_specs=in_specs, out_specs=out_specs, check_vma=False)
```

```python
import jax
import jax.numpy as jnp
from jax import lax
from jax.sharding import PartitionSpec as P

HD = 64


ROPE_BASE = 500000.0
EPSILON = 1e-05
MASKED = -1e30


def rope_tables(positions):
    half_size = HD // 2
    freq_index = jnp.arange(half_size, dtype=jnp.float32)
    inverse = ROPE_BASE ** (-2.0 * freq_index / HD)
    angles = positions.astype(jnp.float32)[..., None] * inverse
    return (jnp.cos(angles)[..., None, :], jnp.sin(angles)[..., None, :])


def rotate(values, tables):
    half_size = values.shape[-1] // 2
    cosine, sine_part = tables
    first_half = values[..., :half_size]
    second = values[..., half_size:]
    return jnp.concatenate(
        [first_half * cosine - second * sine_part, second * cosine + first_half * sine_part],
        axis=-1,
    )


def normalize(hidden_in, steering, gain_row):
    residual = hidden_in.astype(jnp.float32) + steering
    normed = (
        residual
        * lax.rsqrt(jnp.mean(residual * residual, axis=-1, keepdims=True) + EPSILON)
        * gain_row
    ).astype(jnp.bfloat16)
    return (residual, normed)


def attend(projected_in, tables, allowed, query_heads):
    row_count = projected_in.shape[0]
    head_size = HD
    query_cols = query_heads * head_size
    kv_heads = (projected_in.shape[1] - query_cols) // (2 * head_size)
    group_size = query_heads // kv_heads
    queries = projected_in[:, :query_cols].reshape(row_count, query_heads, head_size)
    keyval = projected_in[:, query_cols:]
    key_rows = rotate(
        keyval[:, : kv_heads * head_size].reshape(row_count, kv_heads, head_size), tables
    ).astype(jnp.bfloat16)
    values = (
        keyval[:, kv_heads * head_size :]
        .reshape(row_count, kv_heads, head_size)
        .astype(jnp.bfloat16)
    )
    queries = (
        rotate(queries, tables)
        .astype(jnp.bfloat16)
        .reshape(row_count, kv_heads, group_size, head_size)
    )
    scores = jnp.einsum(
        "rkgd,skd->kgrs", queries, key_rows, preferred_element_type=jnp.float32
    ) * head_size ** (-0.5)
    scores = jnp.where(allowed[None, None], scores, MASKED)
    peak = jnp.max(scores, axis=-1, keepdims=True)
    weights = jnp.exp(scores - peak)
    weights = (weights / jnp.sum(weights, axis=-1, keepdims=True)).astype(jnp.bfloat16)
    mixed_heads = jnp.einsum(
        "kgrs,skd->rkgd", weights, values, preferred_element_type=jnp.float32
    ).astype(jnp.bfloat16)
    return mixed_heads.reshape(row_count, query_heads * head_size)


def project_in(normed, w_qkv):
    return jnp.dot(normed, w_qkv, preferred_element_type=jnp.float32)


def project_out(residual, mixed_heads, w_out):
    return (residual + jnp.dot(mixed_heads, w_out, preferred_element_type=jnp.float32)).astype(
        jnp.bfloat16
    )


def layer_forward(hidden_in, steering, gain_row, w_qkv, w_out, tables, allowed):
    residual, normed = normalize(hidden_in, steering, gain_row)
    projected_in = project_in(normed, w_qkv)
    mixed_heads = attend(projected_in, tables, allowed, w_out.shape[0] // HD)
    return (project_out(residual, mixed_heads, w_out), projected_in)


def layer_backward(
    hidden_in, steering, projected_in, upstream, gain_row, w_qkv, w_out, tables, allowed
):
    query_heads = w_out.shape[0] // HD
    (residual, normed), normalize_pull = jax.vjp(
        lambda h, s: normalize(h, s, gain_row), hidden_in, steering
    )
    mixed_heads, attend_pull = jax.vjp(
        lambda p: attend(p, tables, allowed, query_heads), projected_in
    )
    unused_out, out_pull = jax.vjp(
        lambda r, m: project_out(r, m, w_out), residual, mixed_heads
    )
    grad_residual, grad_mixed = out_pull(upstream)
    (grad_projected,) = attend_pull(grad_mixed)
    unused_proj, in_pull = jax.vjp(lambda n: project_in(n, w_qkv), normed)
    (grad_normed,) = in_pull(grad_projected)
    return normalize_pull((grad_residual, grad_normed))


def butterfly_sum(values, axis):
    count = lax.axis_size(axis)
    index = lax.axis_index(axis)
    stride = 1
    while stride < count:
        fan = 4 if count % (stride * 4) == 0 else 2
        local = (index // stride) % fan
        received = [values]
        for offset in range(1, fan):
            route = [
                (i, (i // (stride * fan)) * stride * fan + ((i // stride) % fan ^ offset) * stride + i % stride)
                for i in range(count)
            ]
            received.append(lax.ppermute(values, axis, route))
        stacked = jnp.stack(received)
        ordered = [lax.dynamic_index_in_dim(stacked, local ^ m, 0, keepdims=False) for m in range(fan)]
        if fan == 4:
            values = (ordered[0] + ordered[1]) + (ordered[2] + ordered[3])
        else:
            values = ordered[0] + ordered[1]
        stride *= fan
    return values


def plan_slots(target, device, row_count, capacity, dp_count):
    target_grid = target.reshape(dp_count, row_count)
    target_dev = target_grid // row_count
    target_off = target_grid % row_count
    row_order = jnp.arange(row_count, dtype=jnp.int32)
    matching = target_dev[:, :, None] == target_dev[:, None, :]
    earlier = row_order[None, :] < row_order[:, None]
    rank_ids = jnp.sum((matching & earlier[None]).astype(jnp.int32), axis=2)
    slot_ids = target_dev * capacity + rank_ids
    own_slot = lax.dynamic_index_in_dim(slot_ids, device, 0, keepdims=False)
    column_ids = jnp.arange(dp_count, dtype=jnp.int32)[:, None] * capacity + rank_ids
    landing = (target_dev == device)[None] & (target_off[None] == row_order[:, None, None])
    source_col = jnp.sum(jnp.where(landing, column_ids[None], 0), axis=(1, 2))
    return (own_slot, source_col)


def pack_rows(source_rows, own_slot, slot_count):
    selector = (jnp.arange(slot_count, dtype=jnp.int32)[:, None] == own_slot[None, :]).astype(
        jnp.bfloat16
    )
    return jnp.dot(selector, source_rows, preferred_element_type=jnp.float32).astype(jnp.bfloat16)


def unpack_rows(arrived, source_col):
    selector = (
        source_col[:, None] == jnp.arange(arrived.shape[0], dtype=jnp.int32)[None, :]
    ).astype(jnp.bfloat16)
    return jnp.dot(selector, arrived, preferred_element_type=jnp.float32).astype(jnp.bfloat16)


def body(resid_in, dest_row, doc_ids, cotangent, gain, steer, w_query, w_keyval, w_out):
    dp_count = lax.axis_size("dp")
    section_count = lax.axis_size("section")
    device = lax.axis_index("dp")
    section_idx = lax.axis_index("section")
    micro_count, row_count, width = resid_in.shape
    capacity = row_count // dp_count + 1
    slot_count = dp_count * capacity
    full_qkv = lax.all_gather(
        jnp.concatenate([w_query[0], w_keyval[0]], axis=1), "dp", axis=0, tiled=True
    )
    full_out = lax.all_gather(w_out[0], "dp", axis=1, tiled=True)
    gain_row = gain[0]
    steering = steer[0]
    plans = [
        plan_slots(dest_row[micro_idx], device, row_count, capacity, dp_count)
        for micro_idx in range(micro_count)
    ]
    packed = jnp.stack(
        [
            pack_rows(resid_in[micro_idx], plans[micro_idx][0], slot_count).reshape(
                dp_count, capacity, width
            )
            for micro_idx in range(micro_count)
        ],
        axis=1,
    )
    arrived = lax.all_to_all(packed, "dp", split_axis=0, concat_axis=0, tiled=True)
    grouped = jnp.stack(
        [
            unpack_rows(arrived[:, micro_idx].reshape(slot_count, width), plans[micro_idx][1])
            for micro_idx in range(micro_count)
        ]
    )
    global_rows = device * row_count + jnp.arange(row_count, dtype=jnp.int32)
    flat_count = micro_count * row_count
    tables = rope_tables((global_rows[None, :] - doc_ids).reshape(flat_count))
    micro_of = jnp.arange(flat_count, dtype=jnp.int32) // row_count
    doc_keys = doc_ids.reshape(flat_count) + micro_of * (dp_count * row_count)
    flat_index = jnp.arange(flat_count, dtype=jnp.int32)
    allowed = (doc_keys[:, None] == doc_keys[None, :]) & (
        flat_index[:, None] >= flat_index[None, :]
    )
    grouped = grouped.reshape(flat_count, width)
    cotangent = cotangent.reshape(flat_count, width)

    def run_layer(hidden_in, steer_vec):
        return layer_forward(hidden_in, steer_vec, gain_row, full_qkv, full_out, tables, allowed)

    zero_block = jnp.zeros((flat_count, width), jnp.bfloat16)
    zero_proj = jnp.zeros((flat_count, full_qkv.shape[1]), jnp.float32)

    def precompute(hidden_in):
        return project_in(normalize(hidden_in, steering, gain_row)[1], full_qkv)
    forward_route = [(i, i + 1) for i in range(section_count - 1)]
    backward_route = [(i + 1, i) for i in range(section_count - 1)]

    def forward_step(carry, unused):
        hidden_in, kept, produced, step = carry
        active = section_idx == step
        kept = jnp.where(active, hidden_in, kept)
        hidden_new = lax.cond(active, lambda: run_layer(hidden_in, steering)[0], lambda: zero_block)
        produced = jnp.where(active, hidden_new, produced)
        sent = lax.ppermute(hidden_new, "section", forward_route)
        return ((sent, kept, produced, step + 1), None)

    (unused_in, kept, produced, unused_step), unused_ys = lax.scan(
        forward_step, (grouped, zero_block, zero_block, jnp.int32(0)), None, length=section_count
    )
    first_saved = lax.cond(
        section_idx == section_count - 1, lambda: precompute(kept), lambda: zero_proj
    )

    def backward_step(carry, unused):
        upstream, grad_sum, step, saved = carry
        active = section_idx == step

        def differentiate():
            return layer_backward(
                kept, steering, saved, upstream, gain_row, full_qkv, full_out, tables, allowed
            )

        grad_in, steer_part = lax.cond(
            active, differentiate, lambda: (zero_block, jnp.zeros_like(steering))
        )
        sent = lax.ppermute(grad_in, "section", backward_route)
        next_saved = lax.cond(
            section_idx == step - 1, lambda: precompute(kept), lambda: zero_proj
        )
        return ((sent, grad_sum + steer_part, step - 1, next_saved), None)

    (unused_grad, grad_sum, unused_step, unused_saved), unused_zs = lax.scan(
        backward_step,
        (cotangent, jnp.zeros_like(steering), jnp.int32(section_count - 1), first_saved),
        None,
        length=section_count,
    )

    total = butterfly_sum(grad_sum, "dp")
    return (produced.reshape(1, micro_count, row_count, width), total[None])


def solution(mesh):
    in_specs = (
        P(None, "dp", None),
        P(),
        P(None, "dp"),
        P(None, "dp", None),
        P("section", None),
        P("section", None),
        P("section", "dp", None),
        P("section", "dp", None),
        P("section", None, "dp"),
    )
    out_specs = (P("section", None, "dp", None), P("section", None))
    return jax.shard_map(body, mesh=mesh, in_specs=in_specs, out_specs=out_specs, check_vma=False)
```

```python
import jax
import jax.numpy as jnp
from jax import lax
from jax.sharding import PartitionSpec as P

HD = 64


ROPE_BASE = 500000.0
EPSILON = 1e-05
MASKED = -1e30


def rope_tables(positions):
    half_size = HD // 2
    freq_index = jnp.arange(half_size, dtype=jnp.float32)
    inverse = ROPE_BASE ** (-2.0 * freq_index / HD)
    angles = positions.astype(jnp.float32)[..., None] * inverse
    return (jnp.cos(angles)[..., None, :], jnp.sin(angles)[..., None, :])


def rotate(values, tables):
    half_size = values.shape[-1] // 2
    cosine, sine_part = tables
    first_half = values[..., :half_size]
    second = values[..., half_size:]
    return jnp.concatenate(
        [first_half * cosine - second * sine_part, second * cosine + first_half * sine_part],
        axis=-1,
    )


def normalize(hidden_in, steering, gain_row):
    residual = hidden_in.astype(jnp.float32) + steering
    normed = (
        residual
        * lax.rsqrt(jnp.mean(residual * residual, axis=-1, keepdims=True) + EPSILON)
        * gain_row
    ).astype(jnp.bfloat16)
    return (residual, normed)


def attend(projected_in, tables, allowed, query_heads):
    row_count = projected_in.shape[0]
    head_size = HD
    query_cols = query_heads * head_size
    kv_heads = (projected_in.shape[1] - query_cols) // (2 * head_size)
    group_size = query_heads // kv_heads
    queries = projected_in[:, :query_cols].reshape(row_count, query_heads, head_size)
    keyval = projected_in[:, query_cols:]
    key_rows = rotate(
        keyval[:, : kv_heads * head_size].reshape(row_count, kv_heads, head_size), tables
    ).astype(jnp.bfloat16)
    values = (
        keyval[:, kv_heads * head_size :]
        .reshape(row_count, kv_heads, head_size)
        .astype(jnp.bfloat16)
    )
    queries = (
        rotate(queries, tables)
        .astype(jnp.bfloat16)
        .reshape(row_count, kv_heads, group_size, head_size)
    )
    scores = jnp.einsum(
        "rkgd,skd->kgrs", queries, key_rows, preferred_element_type=jnp.float32
    ) * head_size ** (-0.5)
    scores = jnp.where(allowed[None, None], scores, MASKED)
    peak = jnp.max(scores, axis=-1, keepdims=True)
    weights = jnp.exp(scores - peak)
    weights = (weights / jnp.sum(weights, axis=-1, keepdims=True)).astype(jnp.bfloat16)
    mixed_heads = jnp.einsum(
        "kgrs,skd->rkgd", weights, values, preferred_element_type=jnp.float32
    ).astype(jnp.bfloat16)
    return mixed_heads.reshape(row_count, query_heads * head_size)


def project_in(normed, w_qkv):
    return jnp.dot(normed, w_qkv, preferred_element_type=jnp.float32)


def project_out(residual, mixed_heads, w_out):
    return (residual + jnp.dot(mixed_heads, w_out, preferred_element_type=jnp.float32)).astype(
        jnp.bfloat16
    )


def layer_forward(hidden_in, steering, gain_row, w_qkv, w_out, tables, allowed):
    residual, normed = normalize(hidden_in, steering, gain_row)
    projected_in = project_in(normed, w_qkv)
    mixed_heads = attend(projected_in, tables, allowed, w_out.shape[0] // HD)
    return (project_out(residual, mixed_heads, w_out), projected_in)


def layer_backward(
    hidden_in, steering, projected_in, upstream, gain_row, w_qkv, w_out, tables, allowed
):
    query_heads = w_out.shape[0] // HD
    (residual, normed), normalize_pull = jax.vjp(
        lambda h, s: normalize(h, s, gain_row), hidden_in, steering
    )
    mixed_heads, attend_pull = jax.vjp(
        lambda p: attend(p, tables, allowed, query_heads), projected_in
    )
    unused_out, out_pull = jax.vjp(
        lambda r, m: project_out(r, m, w_out), residual, mixed_heads
    )
    grad_residual, grad_mixed = out_pull(upstream)
    (grad_projected,) = attend_pull(grad_mixed)
    unused_proj, in_pull = jax.vjp(lambda n: project_in(n, w_qkv), normed)
    (grad_normed,) = in_pull(grad_projected)
    return normalize_pull((grad_residual, grad_normed))


def butterfly_sum(values, axis):
    count = lax.axis_size(axis)
    index = lax.axis_index(axis)
    stride = 1
    while stride < count:
        fan = 4 if count % (stride * 4) == 0 else 2
        local = (index // stride) % fan
        received = [values]
        for offset in range(1, fan):
            route = [
                (i, (i // (stride * fan)) * stride * fan + ((i // stride) % fan ^ offset) * stride + i % stride)
                for i in range(count)
            ]
            received.append(lax.ppermute(values, axis, route))
        stacked = jnp.stack(received)
        ordered = [lax.dynamic_index_in_dim(stacked, local ^ m, 0, keepdims=False) for m in range(fan)]
        if fan == 4:
            values = (ordered[0] + ordered[1]) + (ordered[2] + ordered[3])
        else:
            values = ordered[0] + ordered[1]
        stride *= fan
    return values


def plan_slots(target, device, row_count, capacity, dp_count):
    target_grid = target.reshape(dp_count, row_count)
    target_dev = target_grid // row_count
    target_off = target_grid % row_count
    row_order = jnp.arange(row_count, dtype=jnp.int32)
    matching = target_dev[:, :, None] == target_dev[:, None, :]
    earlier = row_order[None, :] < row_order[:, None]
    rank_ids = jnp.sum((matching & earlier[None]).astype(jnp.int32), axis=2)
    slot_ids = target_dev * capacity + rank_ids
    own_slot = lax.dynamic_index_in_dim(slot_ids, device, 0, keepdims=False)
    column_ids = jnp.arange(dp_count, dtype=jnp.int32)[:, None] * capacity + rank_ids
    landing = (target_dev == device)[None] & (target_off[None] == row_order[:, None, None])
    source_col = jnp.sum(jnp.where(landing, column_ids[None], 0), axis=(1, 2))
    return (own_slot, source_col)


def pack_rows(source_rows, own_slot, slot_count):
    selector = (jnp.arange(slot_count, dtype=jnp.int32)[:, None] == own_slot[None, :]).astype(
        jnp.bfloat16
    )
    return jnp.dot(selector, source_rows, preferred_element_type=jnp.float32).astype(jnp.bfloat16)


def unpack_rows(arrived, source_col):
    selector = (
        source_col[:, None] == jnp.arange(arrived.shape[0], dtype=jnp.int32)[None, :]
    ).astype(jnp.bfloat16)
    return jnp.dot(selector, arrived, preferred_element_type=jnp.float32).astype(jnp.bfloat16)


def body(resid_in, dest_row, doc_ids, cotangent, gain, steer, w_query, w_keyval, w_out):
    dp_count = lax.axis_size("dp")
    section_count = lax.axis_size("section")
    device = lax.axis_index("dp")
    section_idx = lax.axis_index("section")
    micro_count, row_count, width = resid_in.shape
    capacity = row_count // dp_count + 1
    slot_count = dp_count * capacity
    full_qkv = lax.all_gather(
        jnp.concatenate([w_query[0], w_keyval[0]], axis=1), "dp", axis=0, tiled=True
    )
    full_out = lax.all_gather(w_out[0], "dp", axis=1, tiled=True)
    gain_row = gain[0]
    steering = steer[0]
    plans = [
        plan_slots(dest_row[micro_idx], device, row_count, capacity, dp_count)
        for micro_idx in range(micro_count)
    ]
    packed = jnp.stack(
        [
            pack_rows(resid_in[micro_idx], plans[micro_idx][0], slot_count).reshape(
                dp_count, capacity, width
            )
            for micro_idx in range(micro_count)
        ],
        axis=1,
    )
    arrived = lax.all_to_all(packed, "dp", split_axis=0, concat_axis=0, tiled=True)
    grouped = jnp.stack(
        [
            unpack_rows(arrived[:, micro_idx].reshape(slot_count, width), plans[micro_idx][1])
            for micro_idx in range(micro_count)
        ]
    )
    global_rows = device * row_count + jnp.arange(row_count, dtype=jnp.int32)
    flat_count = micro_count * row_count
    tables = rope_tables((global_rows[None, :] - doc_ids).reshape(flat_count))
    micro_of = jnp.arange(flat_count, dtype=jnp.int32) // row_count
    doc_keys = doc_ids.reshape(flat_count) + micro_of * (dp_count * row_count)
    flat_index = jnp.arange(flat_count, dtype=jnp.int32)
    allowed = (doc_keys[:, None] == doc_keys[None, :]) & (
        flat_index[:, None] >= flat_index[None, :]
    )
    grouped = grouped.reshape(flat_count, width)
    cotangent = cotangent.reshape(flat_count, width)

    def run_layer(hidden_in, steer_vec):
        return layer_forward(hidden_in, steer_vec, gain_row, full_qkv, full_out, tables, allowed)

    zero_block = jnp.zeros((flat_count, width), jnp.bfloat16)
    zero_proj = jnp.zeros((flat_count, full_qkv.shape[1]), jnp.float32)

    def precompute(hidden_in):
        return project_in(normalize(hidden_in, steering, gain_row)[1], full_qkv)
    forward_route = [(i, i + 1) for i in range(section_count - 1)]
    backward_route = [(i + 1, i) for i in range(section_count - 1)]

    def forward_step(carry, unused):
        hidden_in, kept, produced, step = carry
        active = section_idx == step
        kept = jnp.where(active, hidden_in, kept)
        hidden_new = lax.cond(active, lambda: run_layer(hidden_in, steering)[0], lambda: zero_block)
        produced = jnp.where(active, hidden_new, produced)
        sent = lax.ppermute(hidden_new, "section", forward_route)
        return ((sent, kept, produced, step + 1), None)

    query_heads = full_out.shape[0] // HD

    def first_front():
        residual, normed = normalize(grouped, steering, gain_row)
        return (residual, attend(project_in(normed, full_qkv), tables, allowed, query_heads))

    lead = section_idx == 0
    first_residual, first_mixed = lax.cond(
        lead,
        first_front,
        lambda: (jnp.zeros((flat_count, width), jnp.float32), jnp.zeros((flat_count, full_out.shape[0]), jnp.bfloat16)),
    )
    first_out = lax.cond(
        lead, lambda: project_out(first_residual, first_mixed, full_out), lambda: zero_block
    )
    first_sent = lax.ppermute(first_out, "section", forward_route)
    (unused_in, kept, produced, unused_step), unused_ys = lax.scan(
        forward_step,
        (first_sent, grouped, first_out, jnp.int32(1)),
        None,
        length=section_count - 1,
    )
    first_saved = lax.cond(
        section_idx == section_count - 1, lambda: precompute(kept), lambda: zero_proj
    )

    def backward_step(carry, unused):
        upstream, grad_sum, step, saved = carry
        active = section_idx == step

        def differentiate():
            return layer_backward(
                kept, steering, saved, upstream, gain_row, full_qkv, full_out, tables, allowed
            )

        grad_in, steer_part = lax.cond(
            active, differentiate, lambda: (zero_block, jnp.zeros_like(steering))
        )
        sent = lax.ppermute(grad_in, "section", backward_route)
        next_saved = lax.cond(
            section_idx == step - 1, lambda: precompute(kept), lambda: zero_proj
        )
        return ((sent, grad_sum + steer_part, step - 1, next_saved), None)

    (unused_grad, grad_sum, unused_step, unused_saved), unused_zs = lax.scan(
        backward_step,
        (cotangent, jnp.zeros_like(steering), jnp.int32(section_count - 1), first_saved),
        None,
        length=section_count,
    )

    total = butterfly_sum(grad_sum, "dp")
    return (produced.reshape(1, micro_count, row_count, width), total[None])


def solution(mesh):
    in_specs = (
        P(None, "dp", None),
        P(),
        P(None, "dp"),
        P(None, "dp", None),
        P("section", None),
        P("section", None),
        P("section", "dp", None),
        P("section", "dp", None),
        P("section", None, "dp"),
    )
    out_specs = (P("section", None, "dp", None), P("section", None))
    return jax.shard_map(body, mesh=mesh, in_specs=in_specs, out_specs=out_specs, check_vma=False)
```
